512 devices in a mesh: pool: 64 (over x, z, core), mp: 8 (over y).
Axes of the slice: x: 4, y: 8, z: 8, core: 2. Of those that a mesh axis runs over, the one named last changes fastest.
Arguments:
- residual_in: bfloat16 [16384, 2048], P('pool', 'mp'), may hold values from -6 to 6
- mlp_branch: bfloat16 [16384, 2048], P('pool'), may hold values from -6 to 6
- norm_gain: float32 [2048], replicated, may hold values from 0.5 to 1.5
- norm_bias: float32 [2048], replicated, may hold values from -3 to 3
- w_qkv: bfloat16 [2048, 3, 2048], P('pool', None, 'mp'), may hold values from -0.125 to 0.125
- qkv_bias: float32 [3, 2048], P(None, 'mp'), may hold values from -3 to 3
- cache_pool: bfloat16 [3072, 2, 32, 2048], P('pool', None, None, 'mp'), as said below
- w_dense: bfloat16 [2048, 2048], P('mp', 'pool'), may hold values from -0.125 to 0.125
- dense_bias: float32 [2048], replicated, may hold values from -3 to 3
- next_gain: float32 [2048], replicated, may hold values from 0.5 to 1.5
- next_bias: float32 [2048], replicated, may hold values from -3 to 3
- w_next: bfloat16 [2048, 3, 2048], P('pool', None, 'mp'), may hold values from -0.125 to 0.125
- next_qkv_bias: float32 [3, 2048], P(None, 'mp'), may hold values from -3 to 3
- token_request: int32 [16384], P('pool'), may hold values from 0 to 255, as said below
- cache_len: int32 [256], P('pool'), may hold values from 0 to 1024, as said below
- block_table: int32 [256, 32], P('pool'), may hold values from 0 to 3071, as said below
Outputs:
- hidden_out: bfloat16 [16384, 2048], P('pool', 'mp')
- next_qkv: bfloat16 [16384, 3, 2048], P('pool', None, 'mp')
The draws below stay inside these ranges and needn't reach their ends.
Inputs may be any that keep to these rules, and one draw needn't show every extreme that they name: `token_request`: the 256 tokens of index i of pool belong to the requests i * 4 to (i+1) * 4 - 1, each request's tokens in one run, in increasing order, each request with at least one token. `cache_len`: 0 for a fresh prompt; some request has exactly 1024. `block_table`: block b is held by index b // 48 of pool; a block may appear in several lists; entries at or past a request's cached blocks are padding. Of the 128 entries of the requests of one index of pool, exactly 2 name blocks held by each index of pool. `cache_pool`: cached keys and values.
All inputs are finite; a program needn't handle non-finite values.
Results may differ from the reference program's by a relative error of at most 0.015.
Values may be sent and summed in bfloat16 or wider, within the bound.
No kernel may reach another device: no remote copies, remote signals or barrier semaphores. Data moves between devices by JAX's collectives and lax.ppermute only.
A program may use at most 128 MiB of HBM per device.

```python
import jax
import jax.numpy as jnp
from jax import lax

HEADS = 32
HEAD_DIM = 64
ROT = 32
D = 2048
TOK_DEV = 256
REQ_DEV = 4
BLK = 32
MAXBLK = 32
BLOCKS_DEV = 48
TOKENS = 16384
REQS = 256
POOL_BLOCKS = 3072
N_POOL = 64


def draw_cache_pool(key, part):
    key_first = jax.random.fold_in(key, 0)
    shape = (POOL_BLOCKS, 2, BLK, D)
    values = jax.random.normal(key_first, shape, jnp.float32)
    return jnp.clip(values, -400.0, 400.0).astype(jnp.bfloat16)


def draw_token_request(key, part):
    holders = TOKENS // TOK_DEV

    def one_holder(holder):
        sub_key = jax.random.fold_in(key, holder)
        cuts = jnp.sort(jax.random.permutation(sub_key, TOK_DEV - 1)[:REQ_DEV - 1] + 1)
        spots = jnp.arange(TOK_DEV, dtype=jnp.int32)
        return jnp.sum((spots[:, None] >= cuts[None, :]).astype(jnp.int32), axis=1) + holder * REQ_DEV
    return jax.vmap(one_holder)(jnp.arange(holders, dtype=jnp.int32)).reshape(-1).astype(jnp.int32)


def draw_cache_len(key, part):
    key_first, key_second, key_third = jax.random.split(key, 3)
    longest = MAXBLK * BLK
    fresh = jax.random.randint(key_first, (REQS,), 0, 3) == 0
    longer = jax.random.randint(key_second, (REQS,), longest // 4, longest + 1)
    lengths = jnp.where(fresh, 0, longer)
    chosen = jax.random.randint(key_third, (), 0, REQS)
    return jnp.where(jnp.arange(REQS) == chosen, longest, lengths).astype(jnp.int32)


def draw_block_table(key, part):
    holders = REQS // REQ_DEV
    entries = REQ_DEV * MAXBLK

    def one_holder(holder):
        sub_key = jax.random.fold_in(jax.random.fold_in(key, 7), holder)
        key_first, key_second = jax.random.split(sub_key)
        owners = jax.random.permutation(key_first, entries) % holders
        spots = jax.random.randint(key_second, (entries,), 0, BLOCKS_DEV)
        return (owners * BLOCKS_DEV + spots).reshape(REQ_DEV, MAXBLK)
    return jax.vmap(one_holder)(jnp.arange(holders, dtype=jnp.int32)).reshape(REQS, MAXBLK).astype(jnp.int32)


def levels(own_key, shape, pieces, least, top_value):
    loudness, own = 1.0, jax.random.fold_in(own_key, 6)
    for position, parts in pieces:
        draws = jnp.exp(jax.random.uniform(jax.random.fold_in(own, position), (parts,), jnp.float32, least / len(pieces), top_value / len(pieces)))
        loudness = loudness * jnp.repeat(draws, shape[position] // parts).reshape([-1 if axis == position else 1 for axis in range(len(shape))])
    return loudness


def normal_values(stream_key, extent, scale, bound, shards=(), held_as=jnp.bfloat16):
    loudness = levels(stream_key, extent, shards, -0.22, 0.18) if shards else 1.0
    values = jax.random.normal(stream_key, extent, jnp.float32) * scale * loudness
    return jnp.minimum(jnp.maximum(values, -bound), bound).astype(held_as)


def setup_inputs(seed: int = 0) -> dict:
    splits = jax.random.split(jax.random.key(seed), 17)
    residual_in = normal_values(splits[0], (TOKENS, D), 1.0, 6.0, ((0, 64), (1, 8)))
    mlp_branch = normal_values(splits[1], (TOKENS, D), 1.0, 6.0, ((0, 64),))
    norm_gain = jnp.clip(1.0 + 0.1 * jax.random.normal(splits[2], (D,), jnp.float32), 0.5, 1.5)
    norm_bias = normal_values(splits[3], (D,), 0.5, 3.0, (), jnp.float32)
    w_qkv = normal_values(splits[4], (D, 3, D), D ** -0.5, 0.125, ((0, 64), (2, 8)))
    qkv_bias = normal_values(splits[5], (3, D), 0.5, 3.0, ((1, 8),), jnp.float32)
    cache_pool = draw_cache_pool(jax.random.fold_in(splits[16], 71), 0)
    w_dense = normal_values(splits[7], (D, D), D ** -0.5, 0.125, ((0, 8), (1, 64)))
    dense_bias = normal_values(splits[8], (D,), 0.5, 3.0, (), jnp.float32)
    next_gain = jnp.clip(1.0 + 0.1 * jax.random.normal(splits[9], (D,), jnp.float32), 0.5, 1.5)
    next_bias = normal_values(splits[10], (D,), 0.5, 3.0, (), jnp.float32)
    w_next = normal_values(splits[11], (D, 3, D), D ** -0.5, 0.125, ((0, 64), (2, 8)))
    next_qkv_bias = normal_values(splits[12], (3, D), 0.5, 3.0, ((1, 8),), jnp.float32)
    token_request = draw_token_request(jax.random.fold_in(splits[16], 71), 0)
    cache_len = draw_cache_len(jax.random.fold_in(splits[16], 71), 0)
    block_table = draw_block_table(jax.random.fold_in(splits[16], 71), 0)
    return dict(residual_in=residual_in, mlp_branch=mlp_branch, norm_gain=norm_gain, norm_bias=norm_bias, w_qkv=w_qkv, qkv_bias=qkv_bias, cache_pool=cache_pool, w_dense=w_dense, dense_bias=dense_bias, next_gain=next_gain, next_bias=next_bias, w_next=w_next, next_qkv_bias=next_qkv_bias, token_request=token_request, cache_len=cache_len, block_table=block_table)


epsilon = 1e-05

def layer_norm(row_data, gain_vec, bias_vec):
    values = row_data.astype(jnp.float32)
    row_mean = lax.optimization_barrier(jnp.mean(values, axis=-1, keepdims=True))
    centered = values - row_mean
    spread = lax.optimization_barrier(jnp.mean(centered * centered, axis=-1, keepdims=True))
    return centered * lax.rsqrt(spread + epsilon) * gain_vec + bias_vec

def rotate(head_rows, positions):
    half_rot = ROT // 2
    inverse = 10000.0 ** (-2.0 * jnp.arange(half_rot, dtype=jnp.float32) / ROT)
    angles = positions.astype(jnp.float32)[:, None] * inverse[None, :]
    cosine = jnp.cos(angles)[:, None, :]
    sine = jnp.sin(angles)[:, None, :]
    lower = head_rows[..., :half_rot]
    upper = head_rows[..., half_rot:ROT]
    return jnp.concatenate([lower * cosine - upper * sine, upper * cosine + lower * sine, head_rows[..., ROT:]], axis=-1)

def run_starts(token_request):
    tok_total = token_request.shape[0]
    token_index = jnp.arange(tok_total, dtype=jnp.int32)
    change = jnp.concatenate([jnp.ones((1,), dtype=bool), token_request[1:] != token_request[:-1]])
    return (token_index, lax.cummax(jnp.where(change, token_index, 0), axis=0))

def block_attention(block_no, query, key_new, value_new, token_request, cache_len, block_table, cache_pool):
    base = block_no * TOK_DEV
    first_req = block_no * REQ_DEV
    q_rows = lax.dynamic_slice_in_dim(query, base, TOK_DEV, 0).astype(jnp.float32)
    k_rows = lax.dynamic_slice_in_dim(key_new, base, TOK_DEV, 0).astype(jnp.float32)
    v_rows = lax.dynamic_slice_in_dim(value_new, base, TOK_DEV, 0).astype(jnp.float32)
    requests = lax.dynamic_slice_in_dim(token_request, base, TOK_DEV, 0)
    table = lax.dynamic_slice_in_dim(block_table, first_req, REQ_DEV, 0).reshape(-1)
    lengths = lax.dynamic_slice_in_dim(cache_len, first_req, REQ_DEV, 0)
    blocks = cache_pool[table].astype(jnp.float32)
    span = MAXBLK * BLK
    slot_total = REQ_DEV * span
    cached_keys = blocks[:, 0].reshape(slot_total, HEADS, HEAD_DIM)
    cached_values = blocks[:, 1].reshape(slot_total, HEADS, HEAD_DIM)
    slot_index = jnp.arange(slot_total, dtype=jnp.int32)
    slot_req = slot_index // span
    slot_len = jnp.repeat(lengths, span, total_repeat_length=slot_total)
    local_req = requests - first_req
    cache_ok = (slot_req[None, :] == local_req[:, None]) & (slot_index % span < slot_len)[None, :]
    token_index = jnp.arange(TOK_DEV, dtype=jnp.int32)
    new_ok = (requests[None, :] == requests[:, None]) & (token_index[None, :] <= token_index[:, None])
    allowed = jnp.concatenate([cache_ok, new_ok], axis=1)
    key_all = jnp.concatenate([cached_keys, k_rows], axis=0)
    value_all = jnp.concatenate([cached_values, v_rows], axis=0)
    score_scale = HEAD_DIM ** (-0.5)
    scores = jnp.einsum('qhd,khd->hqk', q_rows, key_all) * score_scale
    scores = jnp.where(allowed[None], scores, -1e+30)
    row_max = lax.optimization_barrier(jnp.max(scores, axis=-1, keepdims=True))
    weights = jnp.exp(scores - row_max)
    probs = (weights / lax.optimization_barrier(jnp.sum(weights, axis=-1, keepdims=True))).astype(jnp.bfloat16)
    mixed = jnp.einsum('hqk,khd->qhd', probs.astype(jnp.float32), value_all)
    return mixed.reshape(TOK_DEV, D).astype(jnp.bfloat16)

def reference(residual_in, mlp_branch, norm_gain, norm_bias, w_qkv, qkv_bias, cache_pool, w_dense, dense_bias, next_gain, next_bias, w_next, next_qkv_bias, token_request, cache_len, block_table):
    normed = layer_norm(residual_in, norm_gain, norm_bias).astype(jnp.bfloat16)
    projected = jnp.dot(normed, w_qkv.reshape(D, 3 * D), preferred_element_type=jnp.float32).reshape(TOKENS, 3, D) + qkv_bias
    token_index, starts = run_starts(token_request)
    positions = cache_len[token_request] + token_index - starts
    query = rotate(projected[:, 0].reshape(TOKENS, HEADS, HEAD_DIM), positions).astype(jnp.bfloat16)
    key_new = rotate(projected[:, 1].reshape(TOKENS, HEADS, HEAD_DIM), positions).astype(jnp.bfloat16)
    value_new = projected[:, 2].reshape(TOKENS, HEADS, HEAD_DIM).astype(jnp.bfloat16)

    def one_block(block_no):
        return block_attention(block_no, query, key_new, value_new, token_request, cache_len, block_table, cache_pool)
    attended = lax.map(one_block, jnp.arange(N_POOL, dtype=jnp.int32)).reshape(TOKENS, D)
    dense_out = jnp.dot(attended, w_dense, preferred_element_type=jnp.float32) + dense_bias
    hidden_out = (residual_in.astype(jnp.float32) + dense_out + mlp_branch.astype(jnp.float32)).astype(jnp.bfloat16)
    normed_next = layer_norm(hidden_out, next_gain, next_bias).astype(jnp.bfloat16)
    next_raw = jnp.dot(normed_next, w_next.reshape(D, 3 * D), preferred_element_type=jnp.float32).reshape(TOKENS, 3, D) + next_qkv_bias
    return (hidden_out, next_raw.astype(jnp.bfloat16))
```

```python
import jax
import jax.numpy as jnp
from jax import lax
from jax.sharding import PartitionSpec as P

HEAD_DIM = 64
ROT = 32


epsilon = 1e-05


def layer_norm(row_data, gain_vec, bias_vec):
    values = row_data.astype(jnp.float32)
    row_mean = jnp.mean(values, axis=-1, keepdims=True)
    centered = values - row_mean
    spread = jnp.mean(centered * centered, axis=-1, keepdims=True)
    return centered * lax.rsqrt(spread + epsilon) * gain_vec + bias_vec


def rotate(head_rows, positions):
    half_rot = ROT // 2
    inverse = 10000.0 ** (-2.0 * jnp.arange(half_rot, dtype=jnp.float32) / ROT)
    angles = positions.astype(jnp.float32)[:, None] * inverse[None, :]
    cosine = jnp.cos(angles)[:, None, :]
    sine = jnp.sin(angles)[:, None, :]
    lower = head_rows[..., :half_rot]
    upper = head_rows[..., half_rot:ROT]
    return jnp.concatenate(
        [lower * cosine - upper * sine, upper * cosine + lower * sine, head_rows[..., ROT:]],
        axis=-1,
    )


def run_starts(token_request):
    tok_total = token_request.shape[0]
    token_index = jnp.arange(tok_total, dtype=jnp.int32)
    change = jnp.concatenate([jnp.ones((1,), dtype=bool), token_request[1:] != token_request[:-1]])
    return (token_index, lax.cummax(jnp.where(change, token_index, 0), axis=0))


def row_folder(left_rows, running, w_piece):
    columns_part = lax.slice_in_dim(left_rows, 0, w_piece.shape[0], axis=1)
    return running + jnp.dot(
        columns_part, w_piece.reshape(w_piece.shape[0], -1), preferred_element_type=jnp.float32
    )


def local(
    residual_in,
    mlp_branch,
    norm_gain,
    norm_bias,
    w_qkv,
    qkv_bias,
    cache_pool,
    w_dense,
    dense_bias,
    next_gain,
    next_bias,
    w_next,
    next_qkv_bias,
    token_request,
    cache_len,
    block_table,
):
    full_rows = lax.all_gather(residual_in, "mp", axis=1, tiled=True)
    tok_count = full_rows.shape[0]
    col_width = w_qkv.shape[2]
    head_count = col_width // HEAD_DIM
    normed = layer_norm(full_rows, norm_gain, norm_bias).astype(jnp.bfloat16)
    empty_sum = jnp.zeros((tok_count, 3 * col_width), jnp.float32)
    w_rows = w_qkv.shape[0]
    dense_shard = w_dense.reshape(w_rows, -1)
    joined = jnp.concatenate(
        [w_qkv.reshape(w_rows, -1), w_next.reshape(w_rows, -1), dense_shard], axis=1
    )
    gathered = lax.all_gather(joined, "pool", axis=0, tiled=True)
    qkv_cols = 3 * col_width
    w_qkv_full = gathered[:, :qkv_cols]
    w_next_full = gathered[:, qkv_cols : 2 * qkv_cols]
    pool_total = lax.axis_size("pool")
    w_dense_full = (
        gathered[:, 2 * qkv_cols :]
        .reshape((pool_total,) + w_dense.shape)
        .transpose(1, 0, 2)
        .reshape(w_dense.shape[0], -1)
    )
    projected = row_folder(normed, empty_sum, w_qkv_full)
    projected = (projected + qkv_bias.reshape(1, 3 * col_width)).reshape(tok_count, 3, col_width)
    token_index, starts = run_starts(token_request)
    request_count = cache_len.shape[0]
    local_req = token_request - request_count * lax.axis_index("pool")
    request_ids = jnp.arange(request_count, dtype=jnp.int32)
    request_match = local_req[:, None] == request_ids[None, :]
    cached_here = jnp.sum(jnp.where(request_match, cache_len[None, :], 0), axis=1)
    positions = cached_here + token_index - starts
    query = rotate(projected[:, 0].reshape(tok_count, head_count, HEAD_DIM), positions).astype(
        jnp.bfloat16
    )
    key_new = rotate(projected[:, 1].reshape(tok_count, head_count, HEAD_DIM), positions).astype(
        jnp.bfloat16
    )
    value_new = projected[:, 2].reshape(tok_count, head_count, HEAD_DIM).astype(jnp.bfloat16)
    pool_count = lax.axis_size("pool")
    blocks_here = cache_pool.shape[0]
    entries = block_table.reshape(-1)
    holder_order = jnp.argsort(entries // blocks_here, stable=True)
    slot_ids = (entries % blocks_here)[holder_order].reshape(pool_count, -1)
    wanted = lax.all_to_all(slot_ids, "pool", split_axis=0, concat_axis=0, tiled=True)
    packed = cache_pool[wanted.reshape(-1)].reshape((pool_count, -1) + cache_pool.shape[1:])
    arrived = lax.all_to_all(packed, "pool", split_axis=0, concat_axis=0, tiled=True)
    table_blocks = arrived.reshape((-1,) + cache_pool.shape[1:])[jnp.argsort(holder_order)]
    span = block_table.shape[1] * cache_pool.shape[2]
    slot_total = request_count * span
    cached_keys = table_blocks[:, 0].reshape(slot_total, head_count, HEAD_DIM)
    cached_values = table_blocks[:, 1].reshape(slot_total, head_count, HEAD_DIM)
    slot_index = jnp.arange(slot_total, dtype=jnp.int32)
    slot_req = slot_index // span
    slot_len = jnp.repeat(cache_len, span, total_repeat_length=slot_total)
    cache_ok = (slot_req[None, :] == local_req[:, None]) & (slot_index % span < slot_len)[None, :]
    new_ok = (token_request[None, :] == token_request[:, None]) & (
        token_index[None, :] <= token_index[:, None]
    )
    allowed = jnp.concatenate([cache_ok, new_ok], axis=1)
    key_all = jnp.concatenate([cached_keys, key_new], axis=0).transpose(1, 0, 2)
    value_all = jnp.concatenate([cached_values, value_new], axis=0).transpose(1, 0, 2)
    score_scale = HEAD_DIM ** (-0.5)

    def one_head(operands):
        q_head, k_head, v_head = operands
        scores = (
            jnp.einsum("qd,kd->qk", q_head, k_head, preferred_element_type=jnp.float32)
            * score_scale
        )
        scores = jnp.where(allowed, scores, -1e30)
        row_max = jnp.max(scores, axis=1, keepdims=True)
        weights = jnp.exp(scores - row_max)
        probs = (weights / jnp.sum(weights, axis=1, keepdims=True)).astype(jnp.bfloat16)
        return jnp.dot(probs, v_head, preferred_element_type=jnp.float32).astype(jnp.bfloat16)

    mixed = lax.map(one_head, (query.transpose(1, 0, 2), key_all, value_all))
    attended = mixed.transpose(1, 0, 2).reshape(tok_count, col_width)
    partial_out = jnp.dot(
        attended,
        w_dense_full,
        preferred_element_type=jnp.float32,
    )
    mp_index = lax.axis_index("mp")
    dense_total = lax.psum(partial_out.astype(jnp.bfloat16), "mp").astype(jnp.float32)
    whole_hidden = (
        full_rows.astype(jnp.float32) + dense_total + dense_bias + mlp_branch.astype(jnp.float32)
    ).astype(jnp.bfloat16)
    hidden_out = lax.dynamic_slice_in_dim(whole_hidden, mp_index * col_width, col_width, 1)
    normed_next = layer_norm(whole_hidden, next_gain, next_bias).astype(jnp.bfloat16)
    next_raw = row_folder(
        normed_next, empty_sum, w_next_full
    )
    next_qkv = (
        (next_raw + next_qkv_bias.reshape(1, 3 * col_width))
        .astype(jnp.bfloat16)
        .reshape(tok_count, 3, col_width)
    )
    return (hidden_out, next_qkv)


def solution(mesh):
    in_specs = (
        P("pool", "mp"),
        P("pool", None),
        P(),
        P(),
        P("pool", None, "mp"),
        P(None, "mp"),
        P("pool", None, None, "mp"),
        P("mp", "pool"),
        P(),
        P(),
        P(),
        P("pool", None, "mp"),
        P(None, "mp"),
        P("pool"),
        P("pool"),
        P("pool", None),
    )
    out_specs = (P("pool", "mp"), P("pool", None, "mp"))
    return jax.shard_map(local, mesh=mesh, in_specs=in_specs, out_specs=out_specs, check_vma=False)
```

```python
import jax
import jax.numpy as jnp
from jax import lax
from jax.sharding import PartitionSpec as P
from jax.experimental import pallas as pl
from jax.experimental.pallas import tpu as pltpu

HEAD_DIM = 64
ROT = 32


epsilon = 1e-05


def layer_norm(row_data, gain_vec, bias_vec):
    values = row_data.astype(jnp.float32)
    row_mean = jnp.mean(values, axis=-1, keepdims=True)
    centered = values - row_mean
    spread = jnp.mean(centered * centered, axis=-1, keepdims=True)
    return centered * lax.rsqrt(spread + epsilon) * gain_vec + bias_vec


def rotate(head_rows, positions):
    half_rot = ROT // 2
    inverse = 10000.0 ** (-2.0 * jnp.arange(half_rot, dtype=jnp.float32) / ROT)
    angles = positions.astype(jnp.float32)[:, None] * inverse[None, :]
    cosine = jnp.cos(angles)[:, None, :]
    sine = jnp.sin(angles)[:, None, :]
    lower = head_rows[..., :half_rot]
    upper = head_rows[..., half_rot:ROT]
    return jnp.concatenate(
        [lower * cosine - upper * sine, upper * cosine + lower * sine, head_rows[..., ROT:]],
        axis=-1,
    )


def run_starts(token_request):
    tok_total = token_request.shape[0]
    token_index = jnp.arange(tok_total, dtype=jnp.int32)
    change = jnp.concatenate([jnp.ones((1,), dtype=bool), token_request[1:] != token_request[:-1]])
    return (token_index, lax.cummax(jnp.where(change, token_index, 0), axis=0))


def row_folder(left_rows, running, w_piece):
    columns_part = lax.slice_in_dim(left_rows, 0, w_piece.shape[0], axis=1)
    return running + jnp.dot(
        columns_part, w_piece.reshape(w_piece.shape[0], -1), preferred_element_type=jnp.float32
    )


Q_CHUNK = 128
PAIR = 128


def attention_body(q_ref, kc_ref, vc_ref, kn_ref, vn_ref, keyc_ref, keyn_ref, qreq_ref, out_ref):
    chunk = pl.program_id(0)
    n_slots = kc_ref.shape[0] * kc_ref.shape[1] * kc_ref.shape[2]
    n_new = kn_ref.shape[0]
    score_scale = HEAD_DIM ** (-0.5)
    q_req = qreq_ref[...]
    mask_c = q_req == keyc_ref[...]
    row_ids = chunk * Q_CHUNK + lax.broadcasted_iota(jnp.int32, (Q_CHUNK, n_new), 0)
    col_ids = lax.broadcasted_iota(jnp.int32, (Q_CHUNK, n_new), 1)
    mask_n = (q_req == keyn_ref[...]) & (col_ids <= row_ids)
    lane = lax.broadcasted_iota(jnp.int32, (1, PAIR), 1)
    nt = (((1,), (1,)), ((), ()))
    for pair in range(out_ref.shape[1] // PAIR):
        cols = slice(pair * PAIR, (pair + 1) * PAIR)
        q_pair = q_ref[:, cols]
        k_pair = kc_ref[:, :, :, cols].reshape(n_slots, PAIR)
        v_pair = vc_ref[:, :, :, cols].reshape(n_slots, PAIR)
        kn_pair = kn_ref[:, cols]
        vn_pair = vn_ref[:, cols]
        halves = []
        for half in range(PAIR // HEAD_DIM):
            in_head = (lane >= half * HEAD_DIM) & (lane < (half + 1) * HEAD_DIM)
            q_head = jnp.where(in_head, q_pair, jnp.zeros_like(q_pair))
            s_c = lax.dot_general(q_head, k_pair, nt, preferred_element_type=jnp.float32)
            s_n = lax.dot_general(q_head, kn_pair, nt, preferred_element_type=jnp.float32)
            s_c = jnp.where(mask_c, s_c * score_scale, -1e30)
            s_n = jnp.where(mask_n, s_n * score_scale, -1e30)
            row_max = jnp.maximum(
                jnp.max(s_c, axis=1, keepdims=True), jnp.max(s_n, axis=1, keepdims=True)
            )
            w_c = jnp.exp(s_c - row_max)
            w_n = jnp.exp(s_n - row_max)
            total = jnp.sum(w_c, axis=1, keepdims=True) + jnp.sum(w_n, axis=1, keepdims=True)
            p_c = (w_c / total).astype(jnp.bfloat16)
            p_n = (w_n / total).astype(jnp.bfloat16)
            o = jnp.dot(p_c, v_pair, preferred_element_type=jnp.float32) + jnp.dot(
                p_n, vn_pair, preferred_element_type=jnp.float32
            )
            halves.append((in_head, o))
        merged = jnp.where(halves[0][0], halves[0][1], halves[1][1])
        out_ref[:, cols] = merged.astype(out_ref.dtype)


def attention_call(query, arrived, key_new, value_new, key_req_c, key_req_n, q_req):
    tok, width = query.shape
    holders, per, _, blk, _ = arrived.shape
    n_slots = holders * per * blk
    grid = (tok // Q_CHUNK,)
    full = lambda c: (0, 0)
    return pl.pallas_call(
        attention_body,
        grid=grid,
        in_specs=[
            pl.BlockSpec((Q_CHUNK, width), lambda c: (c, 0)),
            pl.BlockSpec((holders, per, None, blk, width), lambda c: (0, 0, 0, 0, 0)),
            pl.BlockSpec((holders, per, None, blk, width), lambda c: (0, 0, 1, 0, 0)),
            pl.BlockSpec((tok, width), full),
            pl.BlockSpec((tok, width), full),
            pl.BlockSpec((1, n_slots), full),
            pl.BlockSpec((1, tok), full),
            pl.BlockSpec((Q_CHUNK, 1), lambda c: (c, 0)),
        ],
        out_specs=pl.BlockSpec((Q_CHUNK, width), lambda c: (c, 0)),
        out_shape=jax.ShapeDtypeStruct((tok, width), jnp.bfloat16),
    )(query, arrived, arrived, key_new, value_new, key_req_c, key_req_n, q_req)


def local(
    residual_in,
    mlp_branch,
    norm_gain,
    norm_bias,
    w_qkv,
    qkv_bias,
    cache_pool,
    w_dense,
    dense_bias,
    next_gain,
    next_bias,
    w_next,
    next_qkv_bias,
    token_request,
    cache_len,
    block_table,
):
    full_rows = lax.all_gather(residual_in, "mp", axis=1, tiled=True)
    tok_count = full_rows.shape[0]
    col_width = w_qkv.shape[2]
    head_count = col_width // HEAD_DIM
    normed = layer_norm(full_rows, norm_gain, norm_bias).astype(jnp.bfloat16)
    empty_sum = jnp.zeros((tok_count, 3 * col_width), jnp.float32)
    w_rows = w_qkv.shape[0]
    dense_shard = w_dense.reshape(w_rows, -1)
    joined = jnp.concatenate(
        [w_qkv.reshape(w_rows, -1), w_next.reshape(w_rows, -1), dense_shard], axis=1
    )
    gathered = lax.all_gather(joined, "pool", axis=0, tiled=True)
    qkv_cols = 3 * col_width
    w_qkv_full = gathered[:, :qkv_cols]
    w_next_full = gathered[:, qkv_cols : 2 * qkv_cols]
    pool_total = lax.axis_size("pool")
    w_dense_full = (
        gathered[:, 2 * qkv_cols :]
        .reshape((pool_total,) + w_dense.shape)
        .transpose(1, 0, 2)
        .reshape(w_dense.shape[0], -1)
    )
    projected = row_folder(normed, empty_sum, w_qkv_full)
    projected = (projected + qkv_bias.reshape(1, 3 * col_width)).reshape(tok_count, 3, col_width)
    token_index, starts = run_starts(token_request)
    request_count = cache_len.shape[0]
    local_req = token_request - request_count * lax.axis_index("pool")
    request_ids = jnp.arange(request_count, dtype=jnp.int32)
    request_match = local_req[:, None] == request_ids[None, :]
    cached_here = jnp.sum(jnp.where(request_match, cache_len[None, :], 0), axis=1)
    positions = cached_here + token_index - starts
    query = rotate(projected[:, 0].reshape(tok_count, head_count, HEAD_DIM), positions).astype(
        jnp.bfloat16
    )
    key_new = rotate(projected[:, 1].reshape(tok_count, head_count, HEAD_DIM), positions).astype(
        jnp.bfloat16
    )
    value_new = projected[:, 2].reshape(tok_count, head_count, HEAD_DIM).astype(jnp.bfloat16)
    pool_count = lax.axis_size("pool")
    blocks_here = cache_pool.shape[0]
    entries = block_table.reshape(-1)
    holder_order = jnp.argsort(entries // blocks_here, stable=True)
    slot_ids = (entries % blocks_here)[holder_order].reshape(pool_count, -1)
    wanted = lax.all_to_all(slot_ids, "pool", split_axis=0, concat_axis=0, tiled=True)
    packed = cache_pool[wanted.reshape(-1)].reshape((pool_count, -1) + cache_pool.shape[1:])
    arrived = lax.all_to_all(packed, "pool", split_axis=0, concat_axis=0, tiled=True)
    span = block_table.shape[1] * cache_pool.shape[2]
    blk_len = cache_pool.shape[2]
    entry_of = holder_order.astype(jnp.int32)
    entry_req = entry_of // block_table.shape[1]
    entry_lim = cache_len[entry_req] - (entry_of % block_table.shape[1]) * blk_len
    pos_in_blk = jnp.arange(blk_len, dtype=jnp.int32)
    key_req_c = jnp.where(
        pos_in_blk[None, :] < entry_lim[:, None], entry_req[:, None], -1
    ).reshape(1, -1)
    attended = attention_call(
        query.reshape(tok_count, col_width),
        arrived,
        key_new.reshape(tok_count, col_width),
        value_new.reshape(tok_count, col_width),
        key_req_c,
        local_req.reshape(1, tok_count),
        local_req.reshape(tok_count, 1),
    )
    partial_out = jnp.dot(
        attended,
        w_dense_full,
        preferred_element_type=jnp.float32,
    )
    mp_index = lax.axis_index("mp")
    dense_total = lax.psum(partial_out.astype(jnp.bfloat16), "mp").astype(jnp.float32)
    whole_hidden = (
        full_rows.astype(jnp.float32) + dense_total + dense_bias + mlp_branch.astype(jnp.float32)
    ).astype(jnp.bfloat16)
    hidden_out = lax.dynamic_slice_in_dim(whole_hidden, mp_index * col_width, col_width, 1)
    normed_next = layer_norm(whole_hidden, next_gain, next_bias).astype(jnp.bfloat16)
    next_raw = row_folder(
        normed_next, empty_sum, w_next_full
    )
    next_qkv = (
        (next_raw + next_qkv_bias.reshape(1, 3 * col_width))
        .astype(jnp.bfloat16)
        .reshape(tok_count, 3, col_width)
    )
    return (hidden_out, next_qkv)


def solution(mesh):
    in_specs = (
        P("pool", "mp"),
        P("pool", None),
        P(),
        P(),
        P("pool", None, "mp"),
        P(None, "mp"),
        P("pool", None, None, "mp"),
        P("mp", "pool"),
        P(),
        P(),
        P(),
        P("pool", None, "mp"),
        P(None, "mp"),
        P("pool"),
        P("pool"),
        P("pool", None),
    )
    out_specs = (P("pool", "mp"), P("pool", None, "mp"))
    return jax.shard_map(local, mesh=mesh, in_specs=in_specs, out_specs=out_specs, check_vma=False)
```

```python
import jax
import jax.numpy as jnp
from jax import lax
from jax.sharding import PartitionSpec as P
from jax.experimental import pallas as pl
from jax.experimental.pallas import tpu as pltpu

HEAD_DIM = 64
ROT = 32


epsilon = 1e-05


def layer_norm(row_data, gain_vec, bias_vec):
    values = row_data.astype(jnp.float32)
    row_mean = jnp.mean(values, axis=-1, keepdims=True)
    centered = values - row_mean
    spread = jnp.mean(centered * centered, axis=-1, keepdims=True)
    return centered * lax.rsqrt(spread + epsilon) * gain_vec + bias_vec


def rotate(head_rows, positions):
    half_rot = ROT // 2
    inverse = 10000.0 ** (-2.0 * jnp.arange(half_rot, dtype=jnp.float32) / ROT)
    angles = positions.astype(jnp.float32)[:, None] * inverse[None, :]
    cosine = jnp.cos(angles)[:, None, :]
    sine = jnp.sin(angles)[:, None, :]
    lower = head_rows[..., :half_rot]
    upper = head_rows[..., half_rot:ROT]
    return jnp.concatenate(
        [lower * cosine - upper * sine, upper * cosine + lower * sine, head_rows[..., ROT:]],
        axis=-1,
    )


def run_starts(token_request):
    tok_total = token_request.shape[0]
    token_index = jnp.arange(tok_total, dtype=jnp.int32)
    change = jnp.concatenate([jnp.ones((1,), dtype=bool), token_request[1:] != token_request[:-1]])
    return (token_index, lax.cummax(jnp.where(change, token_index, 0), axis=0))


def row_folder(left_rows, running, w_piece):
    columns_part = lax.slice_in_dim(left_rows, 0, w_piece.shape[0], axis=1)
    return running + jnp.dot(
        columns_part, w_piece.reshape(w_piece.shape[0], -1), preferred_element_type=jnp.float32
    )


def mp_gather(block, mp_count):
    spread = jnp.broadcast_to(block[None], (mp_count,) + block.shape)
    joined = lax.all_to_all(spread, "mp", split_axis=0, concat_axis=2, tiled=True)
    return joined.reshape(block.shape[0], mp_count * block.shape[1])


Q_CHUNK = 128
PAIR = 128


def attention_body(q_ref, kc_ref, vc_ref, kn_ref, vn_ref, keyc_ref, keyn_ref, qreq_ref, out_ref):
    chunk = pl.program_id(0)
    n_slots = kc_ref.shape[0] * kc_ref.shape[1] * kc_ref.shape[2]
    n_new = kn_ref.shape[0]
    score_scale = HEAD_DIM ** (-0.5)
    q_req = qreq_ref[...]
    mask_c = q_req == keyc_ref[...]
    row_ids = chunk * Q_CHUNK + lax.broadcasted_iota(jnp.int32, (Q_CHUNK, n_new), 0)
    col_ids = lax.broadcasted_iota(jnp.int32, (Q_CHUNK, n_new), 1)
    mask_n = (q_req == keyn_ref[...]) & (col_ids <= row_ids)
    lane = lax.broadcasted_iota(jnp.int32, (1, PAIR), 1)
    nt = (((1,), (1,)), ((), ()))
    for pair in range(out_ref.shape[1] // PAIR):
        cols = slice(pair * PAIR, (pair + 1) * PAIR)
        q_pair = q_ref[:, cols]
        k_pair = kc_ref[:, :, :, cols].reshape(n_slots, PAIR)
        v_pair = vc_ref[:, :, :, cols].reshape(n_slots, PAIR)
        kn_pair = kn_ref[:, cols]
        vn_pair = vn_ref[:, cols]
        halves = []
        for half in range(PAIR // HEAD_DIM):
            in_head = (lane >= half * HEAD_DIM) & (lane < (half + 1) * HEAD_DIM)
            q_head = jnp.where(in_head, q_pair, jnp.zeros_like(q_pair))
            s_c = lax.dot_general(q_head, k_pair, nt, preferred_element_type=jnp.float32)
            s_n = lax.dot_general(q_head, kn_pair, nt, preferred_element_type=jnp.float32)
            s_c = jnp.where(mask_c, s_c * score_scale, -1e30)
            s_n = jnp.where(mask_n, s_n * score_scale, -1e30)
            row_max = jnp.maximum(
                jnp.max(s_c, axis=1, keepdims=True), jnp.max(s_n, axis=1, keepdims=True)
            )
            w_c = jnp.exp(s_c - row_max)
            w_n = jnp.exp(s_n - row_max)
            total = jnp.sum(w_c, axis=1, keepdims=True) + jnp.sum(w_n, axis=1, keepdims=True)
            p_c = (w_c / total).astype(jnp.bfloat16)
            p_n = (w_n / total).astype(jnp.bfloat16)
            o = jnp.dot(p_c, v_pair, preferred_element_type=jnp.float32) + jnp.dot(
                p_n, vn_pair, preferred_element_type=jnp.float32
            )
            halves.append((in_head, o))
        merged = jnp.where(halves[0][0], halves[0][1], halves[1][1])
        out_ref[:, cols] = merged.astype(out_ref.dtype)


def attention_call(query, arrived, key_new, value_new, key_req_c, key_req_n, q_req):
    tok, width = query.shape
    holders, per, _, blk, _ = arrived.shape
    n_slots = holders * per * blk
    grid = (tok // Q_CHUNK,)
    full = lambda c: (0, 0)
    return pl.pallas_call(
        attention_body,
        grid=grid,
        in_specs=[
            pl.BlockSpec((Q_CHUNK, width), lambda c: (c, 0)),
            pl.BlockSpec((holders, per, None, blk, width), lambda c: (0, 0, 0, 0, 0)),
            pl.BlockSpec((holders, per, None, blk, width), lambda c: (0, 0, 1, 0, 0)),
            pl.BlockSpec((tok, width), full),
            pl.BlockSpec((tok, width), full),
            pl.BlockSpec((1, n_slots), full),
            pl.BlockSpec((1, tok), full),
            pl.BlockSpec((Q_CHUNK, 1), lambda c: (c, 0)),
        ],
        out_specs=pl.BlockSpec((Q_CHUNK, width), lambda c: (c, 0)),
        out_shape=jax.ShapeDtypeStruct((tok, width), jnp.bfloat16),
    )(query, arrived, arrived, key_new, value_new, key_req_c, key_req_n, q_req)


def local(
    residual_in,
    mlp_branch,
    norm_gain,
    norm_bias,
    w_qkv,
    qkv_bias,
    cache_pool,
    w_dense,
    dense_bias,
    next_gain,
    next_bias,
    w_next,
    next_qkv_bias,
    token_request,
    cache_len,
    block_table,
):
    mp_count = lax.axis_size("mp")
    full_rows = mp_gather(residual_in, mp_count)
    tok_count = full_rows.shape[0]
    col_width = w_qkv.shape[2]
    head_count = col_width // HEAD_DIM
    normed = layer_norm(full_rows, norm_gain, norm_bias).astype(jnp.bfloat16)
    empty_sum = jnp.zeros((tok_count, 3 * col_width), jnp.float32)
    w_rows = w_qkv.shape[0]
    dense_shard = w_dense.T
    joined = jnp.concatenate(
        [w_qkv.reshape(w_rows, -1), w_next.reshape(w_rows, -1), dense_shard], axis=1
    )
    gathered = lax.all_gather(joined, "pool", axis=0, tiled=True)
    qkv_cols = 3 * col_width
    w_qkv_full = gathered[:, :qkv_cols]
    w_next_full = gathered[:, qkv_cols : 2 * qkv_cols]
    pool_total = lax.axis_size("pool")
    w_dense_t = gathered[:, 2 * qkv_cols :]
    projected = row_folder(normed, empty_sum, w_qkv_full)
    projected = (projected + qkv_bias.reshape(1, 3 * col_width)).reshape(tok_count, 3, col_width)
    token_index, starts = run_starts(token_request)
    request_count = cache_len.shape[0]
    local_req = token_request - request_count * lax.axis_index("pool")
    request_ids = jnp.arange(request_count, dtype=jnp.int32)
    request_match = local_req[:, None] == request_ids[None, :]
    cached_here = jnp.sum(jnp.where(request_match, cache_len[None, :], 0), axis=1)
    positions = cached_here + token_index - starts
    query = rotate(projected[:, 0].reshape(tok_count, head_count, HEAD_DIM), positions).astype(
        jnp.bfloat16
    )
    key_new = rotate(projected[:, 1].reshape(tok_count, head_count, HEAD_DIM), positions).astype(
        jnp.bfloat16
    )
    value_new = projected[:, 2].reshape(tok_count, head_count, HEAD_DIM).astype(jnp.bfloat16)
    pool_count = lax.axis_size("pool")
    blocks_here = cache_pool.shape[0]
    entries = block_table.reshape(-1)
    holder_order = jnp.argsort(entries // blocks_here, stable=True)
    slot_ids = (entries % blocks_here)[holder_order].reshape(pool_count, -1)
    wanted = lax.all_to_all(slot_ids, "pool", split_axis=0, concat_axis=0, tiled=True)
    packed = cache_pool[wanted.reshape(-1)].reshape((pool_count, -1) + cache_pool.shape[1:])
    arrived = lax.all_to_all(packed, "pool", split_axis=0, concat_axis=0, tiled=True)
    span = block_table.shape[1] * cache_pool.shape[2]
    blk_len = cache_pool.shape[2]
    entry_of = holder_order.astype(jnp.int32)
    entry_req = entry_of // block_table.shape[1]
    entry_lim = cache_len[entry_req] - (entry_of % block_table.shape[1]) * blk_len
    pos_in_blk = jnp.arange(blk_len, dtype=jnp.int32)
    key_req_c = jnp.where(
        pos_in_blk[None, :] < entry_lim[:, None], entry_req[:, None], -1
    ).reshape(1, -1)
    attended = attention_call(
        query.reshape(tok_count, col_width),
        arrived,
        key_new.reshape(tok_count, col_width),
        value_new.reshape(tok_count, col_width),
        key_req_c,
        local_req.reshape(1, tok_count),
        local_req.reshape(tok_count, 1),
    )
    partial_out = lax.dot_general(
        attended, w_dense_t, (((1,), (1,)), ((), ())), preferred_element_type=jnp.float32
    )
    mp_index = lax.axis_index("mp")
    pieces = partial_out.astype(jnp.bfloat16).reshape(tok_count, mp_count, col_width)
    arrived_sums = lax.all_to_all(pieces, "mp", split_axis=1, concat_axis=1, tiled=True)
    dense_total = jnp.sum(arrived_sums.astype(jnp.float32), axis=1)
    own_cols = lambda vec: lax.dynamic_slice_in_dim(vec, mp_index * col_width, col_width, 0)
    own_mlp = lax.dynamic_slice_in_dim(mlp_branch, mp_index * col_width, col_width, 1)
    hidden_out = (
        residual_in.astype(jnp.float32)
        + dense_total
        + own_cols(dense_bias)
        + own_mlp.astype(jnp.float32)
    ).astype(jnp.bfloat16)
    whole_hidden = mp_gather(hidden_out, mp_count)
    normed_next = layer_norm(whole_hidden, next_gain, next_bias).astype(jnp.bfloat16)
    next_raw = row_folder(
        normed_next, empty_sum, w_next_full
    )
    next_qkv = (
        (next_raw + next_qkv_bias.reshape(1, 3 * col_width))
        .astype(jnp.bfloat16)
        .reshape(tok_count, 3, col_width)
    )
    return (hidden_out, next_qkv)


def solution(mesh):
    in_specs = (
        P("pool", "mp"),
        P("pool", None),
        P(),
        P(),
        P("pool", None, "mp"),
        P(None, "mp"),
        P("pool", None, None, "mp"),
        P("mp", "pool"),
        P(),
        P(),
        P(),
        P("pool", None, "mp"),
        P(None, "mp"),
        P("pool"),
        P("pool"),
        P("pool", None),
    )
    out_specs = (P("pool", "mp"), P("pool", None, "mp"))
    return jax.shard_map(local, mesh=mesh, in_specs=in_specs, out_specs=out_specs, check_vma=False)
```

```python
import jax
import jax.numpy as jnp
from jax import lax
from jax.sharding import PartitionSpec as P
from jax.experimental import pallas as pl
from jax.experimental.pallas import tpu as pltpu

HEAD_DIM = 64
ROT = 32


epsilon = 1e-05


def layer_norm(row_data, gain_vec, bias_vec):
    values = row_data.astype(jnp.float32)
    row_mean = jnp.mean(values, axis=-1, keepdims=True)
    centered = values - row_mean
    spread = jnp.mean(centered * centered, axis=-1, keepdims=True)
    return centered * lax.rsqrt(spread + epsilon) * gain_vec + bias_vec


def rotate(head_rows, positions):
    half_rot = ROT // 2
    inverse = 10000.0 ** (-2.0 * jnp.arange(half_rot, dtype=jnp.float32) / ROT)
    angles = positions.astype(jnp.float32)[:, None] * inverse[None, :]
    cosine = jnp.cos(angles)[:, None, :]
    sine = jnp.sin(angles)[:, None, :]
    lower = head_rows[..., :half_rot]
    upper = head_rows[..., half_rot:ROT]
    return jnp.concatenate(
        [lower * cosine - upper * sine, upper * cosine + lower * sine, head_rows[..., ROT:]],
        axis=-1,
    )


def run_starts(token_request):
    tok_total = token_request.shape[0]
    token_index = jnp.arange(tok_total, dtype=jnp.int32)
    change = jnp.concatenate([jnp.ones((1,), dtype=bool), token_request[1:] != token_request[:-1]])
    return (token_index, lax.cummax(jnp.where(change, token_index, 0), axis=0))


def row_folder(left_rows, running, w_piece):
    columns_part = lax.slice_in_dim(left_rows, 0, w_piece.shape[0], axis=1)
    return running + jnp.dot(
        columns_part, w_piece.reshape(w_piece.shape[0], -1), preferred_element_type=jnp.float32
    )


def mp_gather(block, mp_count):
    spread = jnp.broadcast_to(block[None], (mp_count,) + block.shape)
    joined = lax.all_to_all(spread, "mp", split_axis=0, concat_axis=2, tiled=True)
    return joined.reshape(block.shape[0], mp_count * block.shape[1])


def mp_permute_gather(block, mp_count):
    mp_index = lax.axis_index("mp")
    moved = [block] + [
        lax.ppermute(block, "mp", [(src, (src + shift) % mp_count) for src in range(mp_count)])
        for shift in range(1, mp_count)
    ]
    stacked = jnp.stack(moved)
    by_source = stacked[(mp_index - jnp.arange(mp_count)) % mp_count]
    return by_source.transpose(1, 0, 2).reshape(block.shape[0], mp_count * block.shape[1])


Q_CHUNK = 128
PAIR = 128


def attention_body(q_ref, kc_ref, vc_ref, kn_ref, vn_ref, keyc_ref, keyn_ref, qreq_ref, out_ref):
    chunk = pl.program_id(0)
    n_slots = kc_ref.shape[0] * kc_ref.shape[1] * kc_ref.shape[2]
    n_new = kn_ref.shape[0]
    score_scale = HEAD_DIM ** (-0.5)
    q_req = qreq_ref[...]
    mask_c = q_req == keyc_ref[...]
    row_ids = chunk * Q_CHUNK + lax.broadcasted_iota(jnp.int32, (Q_CHUNK, n_new), 0)
    col_ids = lax.broadcasted_iota(jnp.int32, (Q_CHUNK, n_new), 1)
    mask_n = (q_req == keyn_ref[...]) & (col_ids <= row_ids)
    lane = lax.broadcasted_iota(jnp.int32, (1, PAIR), 1)
    nt = (((1,), (1,)), ((), ()))
    for pair in range(out_ref.shape[1] // PAIR):
        cols = slice(pair * PAIR, (pair + 1) * PAIR)
        q_pair = q_ref[:, cols]
        k_pair = kc_ref[:, :, :, cols].reshape(n_slots, PAIR)
        v_pair = vc_ref[:, :, :, cols].reshape(n_slots, PAIR)
        kn_pair = kn_ref[:, cols]
        vn_pair = vn_ref[:, cols]
        halves = []
        for half in range(PAIR // HEAD_DIM):
            in_head = (lane >= half * HEAD_DIM) & (lane < (half + 1) * HEAD_DIM)
            q_head = jnp.where(in_head, q_pair, jnp.zeros_like(q_pair))
            s_c = lax.dot_general(q_head, k_pair, nt, preferred_element_type=jnp.float32)
            s_n = lax.dot_general(q_head, kn_pair, nt, preferred_element_type=jnp.float32)
            s_c = jnp.where(mask_c, s_c * score_scale, -1e30)
            s_n = jnp.where(mask_n, s_n * score_scale, -1e30)
            row_max = jnp.maximum(
                jnp.max(s_c, axis=1, keepdims=True), jnp.max(s_n, axis=1, keepdims=True)
            )
            w_c = jnp.exp(s_c - row_max)
            w_n = jnp.exp(s_n - row_max)
            total = jnp.sum(w_c, axis=1, keepdims=True) + jnp.sum(w_n, axis=1, keepdims=True)
            p_c = (w_c / total).astype(jnp.bfloat16)
            p_n = (w_n / total).astype(jnp.bfloat16)
            o = jnp.dot(p_c, v_pair, preferred_element_type=jnp.float32) + jnp.dot(
                p_n, vn_pair, preferred_element_type=jnp.float32
            )
            halves.append((in_head, o))
        merged = jnp.where(halves[0][0], halves[0][1], halves[1][1])
        out_ref[:, cols] = merged.astype(out_ref.dtype)


def attention_call(query, arrived, key_new, value_new, key_req_c, key_req_n, q_req):
    tok, width = query.shape
    holders, per, _, blk, _ = arrived.shape
    n_slots = holders * per * blk
    grid = (tok // Q_CHUNK,)
    full = lambda c: (0, 0)
    return pl.pallas_call(
        attention_body,
        grid=grid,
        in_specs=[
            pl.BlockSpec((Q_CHUNK, width), lambda c: (c, 0)),
            pl.BlockSpec((holders, per, None, blk, width), lambda c: (0, 0, 0, 0, 0)),
            pl.BlockSpec((holders, per, None, blk, width), lambda c: (0, 0, 1, 0, 0)),
            pl.BlockSpec((tok, width), full),
            pl.BlockSpec((tok, width), full),
            pl.BlockSpec((1, n_slots), full),
            pl.BlockSpec((1, tok), full),
            pl.BlockSpec((Q_CHUNK, 1), lambda c: (c, 0)),
        ],
        out_specs=pl.BlockSpec((Q_CHUNK, width), lambda c: (c, 0)),
        out_shape=jax.ShapeDtypeStruct((tok, width), jnp.bfloat16),
    )(query, arrived, arrived, key_new, value_new, key_req_c, key_req_n, q_req)


def local(
    residual_in,
    mlp_branch,
    norm_gain,
    norm_bias,
    w_qkv,
    qkv_bias,
    cache_pool,
    w_dense,
    dense_bias,
    next_gain,
    next_bias,
    w_next,
    next_qkv_bias,
    token_request,
    cache_len,
    block_table,
):
    mp_count = lax.axis_size("mp")
    full_rows = mp_permute_gather(residual_in, mp_count)
    tok_count = full_rows.shape[0]
    col_width = w_qkv.shape[2]
    head_count = col_width // HEAD_DIM
    normed = layer_norm(full_rows, norm_gain, norm_bias).astype(jnp.bfloat16)
    empty_sum = jnp.zeros((tok_count, 3 * col_width), jnp.float32)
    w_rows = w_qkv.shape[0]
    dense_shard = w_dense.T
    joined = jnp.concatenate(
        [w_qkv.reshape(w_rows, -1), w_next.reshape(w_rows, -1), dense_shard], axis=1
    )
    gathered = lax.all_gather(joined, "pool", axis=0, tiled=True)
    qkv_cols = 3 * col_width
    w_qkv_full = gathered[:, :qkv_cols]
    w_next_full = gathered[:, qkv_cols : 2 * qkv_cols]
    pool_total = lax.axis_size("pool")
    w_dense_t = gathered[:, 2 * qkv_cols :]
    projected = row_folder(normed, empty_sum, w_qkv_full)
    projected = (projected + qkv_bias.reshape(1, 3 * col_width)).reshape(tok_count, 3, col_width)
    token_index, starts = run_starts(token_request)
    request_count = cache_len.shape[0]
    local_req = token_request - request_count * lax.axis_index("pool")
    request_ids = jnp.arange(request_count, dtype=jnp.int32)
    request_match = local_req[:, None] == request_ids[None, :]
    cached_here = jnp.sum(jnp.where(request_match, cache_len[None, :], 0), axis=1)
    positions = cached_here + token_index - starts
    query = rotate(projected[:, 0].reshape(tok_count, head_count, HEAD_DIM), positions).astype(
        jnp.bfloat16
    )
    key_new = rotate(projected[:, 1].reshape(tok_count, head_count, HEAD_DIM), positions).astype(
        jnp.bfloat16
    )
    value_new = projected[:, 2].reshape(tok_count, head_count, HEAD_DIM).astype(jnp.bfloat16)
    pool_count = lax.axis_size("pool")
    blocks_here = cache_pool.shape[0]
    entries = block_table.reshape(-1)
    holder_order = jnp.argsort(entries // blocks_here, stable=True)
    slot_ids = (entries % blocks_here)[holder_order].reshape(pool_count, -1)
    wanted = lax.all_to_all(slot_ids, "pool", split_axis=0, concat_axis=0, tiled=True)
    packed = cache_pool[wanted.reshape(-1)].reshape((pool_count, -1) + cache_pool.shape[1:])
    arrived = lax.all_to_all(packed, "pool", split_axis=0, concat_axis=0, tiled=True)
    span = block_table.shape[1] * cache_pool.shape[2]
    blk_len = cache_pool.shape[2]
    entry_of = holder_order.astype(jnp.int32)
    entry_req = entry_of // block_table.shape[1]
    entry_lim = cache_len[entry_req] - (entry_of % block_table.shape[1]) * blk_len
    pos_in_blk = jnp.arange(blk_len, dtype=jnp.int32)
    key_req_c = jnp.where(
        pos_in_blk[None, :] < entry_lim[:, None], entry_req[:, None], -1
    ).reshape(1, -1)
    attended = attention_call(
        query.reshape(tok_count, col_width),
        arrived,
        key_new.reshape(tok_count, col_width),
        value_new.reshape(tok_count, col_width),
        key_req_c,
        local_req.reshape(1, tok_count),
        local_req.reshape(tok_count, 1),
    )
    partial_out = lax.dot_general(
        attended, w_dense_t, (((1,), (1,)), ((), ())), preferred_element_type=jnp.float32
    )
    mp_index = lax.axis_index("mp")
    pieces = partial_out.astype(jnp.bfloat16).reshape(tok_count, mp_count, col_width)
    arrived_sums = lax.all_to_all(pieces, "mp", split_axis=1, concat_axis=1, tiled=True)
    dense_total = jnp.sum(arrived_sums.astype(jnp.float32), axis=1)
    own_cols = lambda vec: lax.dynamic_slice_in_dim(vec, mp_index * col_width, col_width, 0)
    own_mlp = lax.dynamic_slice_in_dim(mlp_branch, mp_index * col_width, col_width, 1)
    hidden_out = (
        residual_in.astype(jnp.float32)
        + dense_total
        + own_cols(dense_bias)
        + own_mlp.astype(jnp.float32)
    ).astype(jnp.bfloat16)
    whole_hidden = mp_gather(hidden_out, mp_count)
    normed_next = layer_norm(whole_hidden, next_gain, next_bias).astype(jnp.bfloat16)
    next_raw = row_folder(
        normed_next, empty_sum, w_next_full
    )
    next_qkv = (
        (next_raw + next_qkv_bias.reshape(1, 3 * col_width))
        .astype(jnp.bfloat16)
        .reshape(tok_count, 3, col_width)
    )
    return (hidden_out, next_qkv)


def solution(mesh):
    in_specs = (
        P("pool", "mp"),
        P("pool", None),
        P(),
        P(),
        P("pool", None, "mp"),
        P(None, "mp"),
        P("pool", None, None, "mp"),
        P("mp", "pool"),
        P(),
        P(),
        P(),
        P("pool", None, "mp"),
        P(None, "mp"),
        P("pool"),
        P("pool"),
        P("pool", None),
    )
    out_specs = (P("pool", "mp"), P("pool", None, "mp"))
    return jax.shard_map(local, mesh=mesh, in_specs=in_specs, out_specs=out_specs, check_vma=False)
```

```python
import jax
import jax.numpy as jnp
from jax import lax
from jax.sharding import PartitionSpec as P
from jax.experimental import pallas as pl
from jax.experimental.pallas import tpu as pltpu

HEAD_DIM = 64
ROT = 32


epsilon = 1e-05


def layer_norm(row_data, gain_vec, bias_vec):
    values = row_data.astype(jnp.float32)
    row_mean = jnp.mean(values, axis=-1, keepdims=True)
    centered = values - row_mean
    spread = jnp.mean(centered * centered, axis=-1, keepdims=True)
    return centered * lax.rsqrt(spread + epsilon) * gain_vec + bias_vec


def rotate(head_rows, positions):
    half_rot = ROT // 2
    inverse = 10000.0 ** (-2.0 * jnp.arange(half_rot, dtype=jnp.float32) / ROT)
    angles = positions.astype(jnp.float32)[:, None] * inverse[None, :]
    cosine = jnp.cos(angles)[:, None, :]
    sine = jnp.sin(angles)[:, None, :]
    lower = head_rows[..., :half_rot]
    upper = head_rows[..., half_rot:ROT]
    return jnp.concatenate(
        [lower * cosine - upper * sine, upper * cosine + lower * sine, head_rows[..., ROT:]],
        axis=-1,
    )


def run_starts(token_request):
    tok_total = token_request.shape[0]
    token_index = jnp.arange(tok_total, dtype=jnp.int32)
    change = jnp.concatenate([jnp.ones((1,), dtype=bool), token_request[1:] != token_request[:-1]])
    return (token_index, lax.cummax(jnp.where(change, token_index, 0), axis=0))


def row_folder(left_rows, running, w_piece):
    columns_part = lax.slice_in_dim(left_rows, 0, w_piece.shape[0], axis=1)
    return running + jnp.dot(
        columns_part, w_piece.reshape(w_piece.shape[0], -1), preferred_element_type=jnp.float32
    )


def mp_gather(block, mp_count):
    spread = jnp.broadcast_to(block[None], (mp_count,) + block.shape)
    joined = lax.all_to_all(spread, "mp", split_axis=0, concat_axis=2, tiled=True)
    return joined.reshape(block.shape[0], mp_count * block.shape[1])


def mp_permute_gather(block, mp_count):
    mp_index = lax.axis_index("mp")
    moved = [block] + [
        lax.ppermute(block, "mp", [(src, (src + shift) % mp_count) for src in range(mp_count)])
        for shift in range(1, mp_count)
    ]
    stacked = jnp.stack(moved)
    by_source = stacked[(mp_index - jnp.arange(mp_count)) % mp_count]
    return by_source.transpose(1, 0, 2).reshape(block.shape[0], mp_count * block.shape[1])


Q_CHUNK = 128
PAIR = 128


def attention_body(q_ref, kc_ref, vc_ref, kn_ref, vn_ref, keyc_ref, keyn_ref, qreq_ref, out_ref):
    chunk = pl.program_id(0)
    n_slots = kc_ref.shape[0] * kc_ref.shape[1] * kc_ref.shape[2]
    n_new = kn_ref.shape[0]
    score_scale = HEAD_DIM ** (-0.5)
    q_req = qreq_ref[...]
    mask_c = q_req == keyc_ref[...]
    row_ids = chunk * Q_CHUNK + lax.broadcasted_iota(jnp.int32, (Q_CHUNK, n_new), 0)
    col_ids = lax.broadcasted_iota(jnp.int32, (Q_CHUNK, n_new), 1)
    mask_n = (q_req == keyn_ref[...]) & (col_ids <= row_ids)
    lane = lax.broadcasted_iota(jnp.int32, (1, PAIR), 1)
    nt = (((1,), (1,)), ((), ()))
    for pair in range(out_ref.shape[1] // PAIR):
        cols = slice(pair * PAIR, (pair + 1) * PAIR)
        q_pair = q_ref[:, cols]
        k_pair = kc_ref[:, :, :, cols].reshape(n_slots, PAIR)
        v_pair = vc_ref[:, :, :, cols].reshape(n_slots, PAIR)
        kn_pair = kn_ref[:, cols]
        vn_pair = vn_ref[:, cols]
        halves = []
        for half in range(PAIR // HEAD_DIM):
            in_head = (lane >= half * HEAD_DIM) & (lane < (half + 1) * HEAD_DIM)
            q_head = jnp.where(in_head, q_pair, jnp.zeros_like(q_pair))
            s_c = lax.dot_general(q_head, k_pair, nt, preferred_element_type=jnp.float32)
            s_n = lax.dot_general(q_head, kn_pair, nt, preferred_element_type=jnp.float32)
            s_c = jnp.where(mask_c, s_c * score_scale, -1e30)
            s_n = jnp.where(mask_n, s_n * score_scale, -1e30)
            row_max = jnp.maximum(
                jnp.max(s_c, axis=1, keepdims=True), jnp.max(s_n, axis=1, keepdims=True)
            )
            w_c = jnp.exp(s_c - row_max)
            w_n = jnp.exp(s_n - row_max)
            total = jnp.sum(w_c, axis=1, keepdims=True) + jnp.sum(w_n, axis=1, keepdims=True)
            p_c = (w_c / total).astype(jnp.bfloat16)
            p_n = (w_n / total).astype(jnp.bfloat16)
            o = jnp.dot(p_c, v_pair, preferred_element_type=jnp.float32) + jnp.dot(
                p_n, vn_pair, preferred_element_type=jnp.float32
            )
            halves.append((in_head, o))
        merged = jnp.where(halves[0][0], halves[0][1], halves[1][1])
        out_ref[:, cols] = merged.astype(out_ref.dtype)


def attention_call(query, arrived, key_new, value_new, key_req_c, key_req_n, q_req):
    tok, width = query.shape
    holders, per, _, blk, _ = arrived.shape
    n_slots = holders * per * blk
    grid = (tok // Q_CHUNK,)
    full = lambda c: (0, 0)
    return pl.pallas_call(
        attention_body,
        grid=grid,
        in_specs=[
            pl.BlockSpec((Q_CHUNK, width), lambda c: (c, 0)),
            pl.BlockSpec((holders, per, None, blk, width), lambda c: (0, 0, 0, 0, 0)),
            pl.BlockSpec((holders, per, None, blk, width), lambda c: (0, 0, 1, 0, 0)),
            pl.BlockSpec((tok, width), full),
            pl.BlockSpec((tok, width), full),
            pl.BlockSpec((1, n_slots), full),
            pl.BlockSpec((1, tok), full),
            pl.BlockSpec((Q_CHUNK, 1), lambda c: (c, 0)),
        ],
        out_specs=pl.BlockSpec((Q_CHUNK, width), lambda c: (c, 0)),
        out_shape=jax.ShapeDtypeStruct((tok, width), jnp.bfloat16),
    )(query, arrived, arrived, key_new, value_new, key_req_c, key_req_n, q_req)


def local(
    residual_in,
    mlp_branch,
    norm_gain,
    norm_bias,
    w_qkv,
    qkv_bias,
    cache_pool,
    w_dense,
    dense_bias,
    next_gain,
    next_bias,
    w_next,
    next_qkv_bias,
    token_request,
    cache_len,
    block_table,
):
    mp_count = lax.axis_size("mp")
    full_rows = mp_permute_gather(residual_in, mp_count)
    tok_count = full_rows.shape[0]
    col_width = w_qkv.shape[2]
    head_count = col_width // HEAD_DIM
    normed = layer_norm(full_rows, norm_gain, norm_bias).astype(jnp.bfloat16)
    empty_sum = jnp.zeros((tok_count, 3 * col_width), jnp.float32)
    w_rows = w_qkv.shape[0]
    dense_shard = mp_permute_gather(w_dense.T, mp_count)
    joined = jnp.concatenate(
        [w_qkv.reshape(w_rows, -1), w_next.reshape(w_rows, -1), dense_shard], axis=1
    )
    gathered = lax.all_gather(joined, "pool", axis=0, tiled=True)
    qkv_cols = 3 * col_width
    w_qkv_full = gathered[:, :qkv_cols]
    w_next_full = gathered[:, qkv_cols : 2 * qkv_cols]
    pool_total = lax.axis_size("pool")
    w_dense_t = gathered[:, 2 * qkv_cols :]
    projected = row_folder(normed, empty_sum, w_qkv_full)
    projected = (projected + qkv_bias.reshape(1, 3 * col_width)).reshape(tok_count, 3, col_width)
    token_index, starts = run_starts(token_request)
    request_count = cache_len.shape[0]
    local_req = token_request - request_count * lax.axis_index("pool")
    request_ids = jnp.arange(request_count, dtype=jnp.int32)
    request_match = local_req[:, None] == request_ids[None, :]
    cached_here = jnp.sum(jnp.where(request_match, cache_len[None, :], 0), axis=1)
    positions = cached_here + token_index - starts
    query = rotate(projected[:, 0].reshape(tok_count, head_count, HEAD_DIM), positions).astype(
        jnp.bfloat16
    )
    key_new = rotate(projected[:, 1].reshape(tok_count, head_count, HEAD_DIM), positions).astype(
        jnp.bfloat16
    )
    value_new = projected[:, 2].reshape(tok_count, head_count, HEAD_DIM).astype(jnp.bfloat16)
    pool_count = lax.axis_size("pool")
    blocks_here = cache_pool.shape[0]
    entries = block_table.reshape(-1)
    holder_order = jnp.argsort(entries // blocks_here, stable=True)
    slot_ids = (entries % blocks_here)[holder_order].reshape(pool_count, -1)
    wanted = lax.all_to_all(slot_ids, "pool", split_axis=0, concat_axis=0, tiled=True)
    packed = cache_pool[wanted.reshape(-1)].reshape((pool_count, -1) + cache_pool.shape[1:])
    arrived = lax.all_to_all(packed, "pool", split_axis=0, concat_axis=0, tiled=True)
    span = block_table.shape[1] * cache_pool.shape[2]
    blk_len = cache_pool.shape[2]
    entry_of = holder_order.astype(jnp.int32)
    entry_req = entry_of // block_table.shape[1]
    entry_lim = cache_len[entry_req] - (entry_of % block_table.shape[1]) * blk_len
    pos_in_blk = jnp.arange(blk_len, dtype=jnp.int32)
    key_req_c = jnp.where(
        pos_in_blk[None, :] < entry_lim[:, None], entry_req[:, None], -1
    ).reshape(1, -1)
    attended = attention_call(
        query.reshape(tok_count, col_width),
        arrived,
        key_new.reshape(tok_count, col_width),
        value_new.reshape(tok_count, col_width),
        key_req_c,
        local_req.reshape(1, tok_count),
        local_req.reshape(tok_count, 1),
    )
    mp_index = lax.axis_index("mp")
    whole_dense = lax.dot_general(
        mp_gather(attended, mp_count),
        w_dense_t,
        (((1,), (1,)), ((), ())),
        preferred_element_type=jnp.float32,
    )
    whole_hidden = (
        full_rows.astype(jnp.float32) + whole_dense + dense_bias + mlp_branch.astype(jnp.float32)
    ).astype(jnp.bfloat16)
    hidden_out = lax.dynamic_slice_in_dim(whole_hidden, mp_index * col_width, col_width, 1)
    normed_next = layer_norm(whole_hidden, next_gain, next_bias).astype(jnp.bfloat16)
    next_raw = row_folder(
        normed_next, empty_sum, w_next_full
    )
    next_qkv = (
        (next_raw + next_qkv_bias.reshape(1, 3 * col_width))
        .astype(jnp.bfloat16)
        .reshape(tok_count, 3, col_width)
    )
    return (hidden_out, next_qkv)


def solution(mesh):
    in_specs = (
        P("pool", "mp"),
        P("pool", None),
        P(),
        P(),
        P("pool", None, "mp"),
        P(None, "mp"),
        P("pool", None, None, "mp"),
        P("mp", "pool"),
        P(),
        P(),
        P(),
        P("pool", None, "mp"),
        P(None, "mp"),
        P("pool"),
        P("pool"),
        P("pool", None),
    )
    out_specs = (P("pool", "mp"), P("pool", None, "mp"))
    return jax.shard_map(local, mesh=mesh, in_specs=in_specs, out_specs=out_specs, check_vma=False)
```

```python
import functools

import jax
import jax.numpy as jnp
from jax import lax
from jax.sharding import PartitionSpec as P
from jax.experimental import pallas as pl
from jax.experimental.pallas import tpu as pltpu

HEAD_DIM = 64
ROT = 32


epsilon = 1e-05


def layer_norm(row_data, gain_vec, bias_vec):
    values = row_data.astype(jnp.float32)
    row_mean = jnp.mean(values, axis=-1, keepdims=True)
    centered = values - row_mean
    spread = jnp.mean(centered * centered, axis=-1, keepdims=True)
    return centered * lax.rsqrt(spread + epsilon) * gain_vec + bias_vec


def rotate(head_rows, positions):
    half_rot = ROT // 2
    inverse = 10000.0 ** (-2.0 * jnp.arange(half_rot, dtype=jnp.float32) / ROT)
    angles = positions.astype(jnp.float32)[:, None] * inverse[None, :]
    cosine = jnp.cos(angles)[:, None, :]
    sine = jnp.sin(angles)[:, None, :]
    lower = head_rows[..., :half_rot]
    upper = head_rows[..., half_rot:ROT]
    return jnp.concatenate(
        [lower * cosine - upper * sine, upper * cosine + lower * sine, head_rows[..., ROT:]],
        axis=-1,
    )


def run_starts(token_request):
    tok_total = token_request.shape[0]
    token_index = jnp.arange(tok_total, dtype=jnp.int32)
    change = jnp.concatenate([jnp.ones((1,), dtype=bool), token_request[1:] != token_request[:-1]])
    return (token_index, lax.cummax(jnp.where(change, token_index, 0), axis=0))


def row_folder(left_rows, running, w_piece):
    columns_part = lax.slice_in_dim(left_rows, 0, w_piece.shape[0], axis=1)
    return running + jnp.dot(
        columns_part, w_piece.reshape(w_piece.shape[0], -1), preferred_element_type=jnp.float32
    )


def mp_gather(block, mp_count):
    spread = jnp.broadcast_to(block[None], (mp_count,) + block.shape)
    joined = lax.all_to_all(spread, "mp", split_axis=0, concat_axis=2, tiled=True)
    return joined.reshape(block.shape[0], mp_count * block.shape[1])


def mp_permute_gather(block, mp_count):
    mp_index = lax.axis_index("mp")
    moved = [block] + [
        lax.ppermute(block, "mp", [(src, (src + shift) % mp_count) for src in range(mp_count)])
        for shift in range(1, mp_count)
    ]
    stacked = jnp.stack(moved)
    by_source = stacked[(mp_index - jnp.arange(mp_count)) % mp_count]
    return by_source.transpose(1, 0, 2).reshape(block.shape[0], mp_count * block.shape[1])


Q_CHUNK = 128
PAIR = 128


def attention_body(chunk, q_ref, kc_ref, vc_ref, kn_ref, vn_ref, keyc_ref, keyn_ref, qreq_ref, out_ref):
    n_slots = kc_ref.shape[0] * kc_ref.shape[1] * kc_ref.shape[2]
    n_new = kn_ref.shape[0]
    score_scale = HEAD_DIM ** (-0.5)
    q_req = qreq_ref[...]
    mask_c = q_req == keyc_ref[...]
    row_ids = chunk * Q_CHUNK + lax.broadcasted_iota(jnp.int32, (Q_CHUNK, n_new), 0)
    col_ids = lax.broadcasted_iota(jnp.int32, (Q_CHUNK, n_new), 1)
    mask_n = (q_req == keyn_ref[...]) & (col_ids <= row_ids)
    lane = lax.broadcasted_iota(jnp.int32, (1, PAIR), 1)
    nt = (((1,), (1,)), ((), ()))
    for pair in range(out_ref.shape[1] // PAIR):
        cols = slice(pair * PAIR, (pair + 1) * PAIR)
        q_pair = q_ref[:, cols]
        k_pair = kc_ref[:, :, :, cols].reshape(n_slots, PAIR)
        v_pair = vc_ref[:, :, :, cols].reshape(n_slots, PAIR)
        kn_pair = kn_ref[:, cols]
        vn_pair = vn_ref[:, cols]
        halves = []
        for half in range(PAIR // HEAD_DIM):
            in_head = (lane >= half * HEAD_DIM) & (lane < (half + 1) * HEAD_DIM)
            q_head = jnp.where(in_head, q_pair, jnp.zeros_like(q_pair))
            s_c = lax.dot_general(q_head, k_pair, nt, preferred_element_type=jnp.float32)
            s_n = lax.dot_general(q_head, kn_pair, nt, preferred_element_type=jnp.float32)
            s_c = jnp.where(mask_c, s_c * score_scale, -1e30)
            s_n = jnp.where(mask_n, s_n * score_scale, -1e30)
            row_max = jnp.maximum(
                jnp.max(s_c, axis=1, keepdims=True), jnp.max(s_n, axis=1, keepdims=True)
            )
            w_c = jnp.exp(s_c - row_max)
            w_n = jnp.exp(s_n - row_max)
            total = jnp.sum(w_c, axis=1, keepdims=True) + jnp.sum(w_n, axis=1, keepdims=True)
            p_c = (w_c / total).astype(jnp.bfloat16)
            p_n = (w_n / total).astype(jnp.bfloat16)
            o = jnp.dot(p_c, v_pair, preferred_element_type=jnp.float32) + jnp.dot(
                p_n, vn_pair, preferred_element_type=jnp.float32
            )
            halves.append((in_head, o))
        merged = jnp.where(halves[0][0], halves[0][1], halves[1][1])
        out_ref[:, cols] = merged.astype(out_ref.dtype)


def attention_call(chunk, query, arrived, key_new, value_new, key_req_c, key_req_n, q_req):
    tok, width = query.shape
    holders, per, _, blk, _ = arrived.shape
    n_slots = holders * per * blk
    grid = (1,)
    full = lambda c: (0, 0)
    return pl.pallas_call(
        functools.partial(attention_body, chunk),
        grid=grid,
        in_specs=[
            pl.BlockSpec((Q_CHUNK, width), lambda c: (chunk, 0)),
            pl.BlockSpec((holders, per, None, blk, width), lambda c: (0, 0, 0, 0, 0)),
            pl.BlockSpec((holders, per, None, blk, width), lambda c: (0, 0, 1, 0, 0)),
            pl.BlockSpec((tok, width), full),
            pl.BlockSpec((tok, width), full),
            pl.BlockSpec((1, n_slots), full),
            pl.BlockSpec((1, tok), full),
            pl.BlockSpec((Q_CHUNK, 1), lambda c: (chunk, 0)),
        ],
        out_specs=pl.BlockSpec((Q_CHUNK, width), lambda c: (0, 0)),
        out_shape=jax.ShapeDtypeStruct((Q_CHUNK, width), jnp.bfloat16),
    )(query, arrived, arrived, key_new, value_new, key_req_c, key_req_n, q_req)


def local(
    residual_in,
    mlp_branch,
    norm_gain,
    norm_bias,
    w_qkv,
    qkv_bias,
    cache_pool,
    w_dense,
    dense_bias,
    next_gain,
    next_bias,
    w_next,
    next_qkv_bias,
    token_request,
    cache_len,
    block_table,
):
    mp_count = lax.axis_size("mp")
    full_rows = mp_permute_gather(residual_in, mp_count)
    tok_count = full_rows.shape[0]
    col_width = w_qkv.shape[2]
    head_count = col_width // HEAD_DIM
    normed = layer_norm(full_rows, norm_gain, norm_bias).astype(jnp.bfloat16)
    empty_sum = jnp.zeros((tok_count, 3 * col_width), jnp.float32)
    w_rows = w_qkv.shape[0]
    dense_shard = w_dense.T
    joined = jnp.concatenate(
        [w_qkv.reshape(w_rows, -1), w_next.reshape(w_rows, -1), dense_shard], axis=1
    )
    gathered = lax.all_gather(joined, "pool", axis=0, tiled=True)
    qkv_cols = 3 * col_width
    w_qkv_full = gathered[:, :qkv_cols]
    w_next_full = gathered[:, qkv_cols : 2 * qkv_cols]
    pool_total = lax.axis_size("pool")
    w_dense_t = gathered[:, 2 * qkv_cols :]
    projected = row_folder(normed, empty_sum, w_qkv_full)
    projected = (projected + qkv_bias.reshape(1, 3 * col_width)).reshape(tok_count, 3, col_width)
    token_index, starts = run_starts(token_request)
    request_count = cache_len.shape[0]
    local_req = token_request - request_count * lax.axis_index("pool")
    request_ids = jnp.arange(request_count, dtype=jnp.int32)
    request_match = local_req[:, None] == request_ids[None, :]
    cached_here = jnp.sum(jnp.where(request_match, cache_len[None, :], 0), axis=1)
    positions = cached_here + token_index - starts
    query = rotate(projected[:, 0].reshape(tok_count, head_count, HEAD_DIM), positions).astype(
        jnp.bfloat16
    )
    key_new = rotate(projected[:, 1].reshape(tok_count, head_count, HEAD_DIM), positions).astype(
        jnp.bfloat16
    )
    value_new = projected[:, 2].reshape(tok_count, head_count, HEAD_DIM).astype(jnp.bfloat16)
    pool_count = lax.axis_size("pool")
    blocks_here = cache_pool.shape[0]
    entries = block_table.reshape(-1)
    holder = entries // blocks_here
    entry_ids = jnp.arange(entries.shape[0], dtype=jnp.int32)
    earlier_same = (holder[:, None] == holder[None, :]) & (entry_ids[None, :] < entry_ids[:, None])
    per_holder = entries.shape[0] // pool_count
    slot_of = holder * per_holder + jnp.sum(earlier_same.astype(jnp.int32), axis=1)
    placed = slot_of[:, None] == entry_ids[None, :]
    holder_order = jnp.sum(jnp.where(placed, entry_ids[:, None], 0), axis=0)
    slot_ids = jnp.sum(jnp.where(placed, (entries % blocks_here)[:, None], 0), axis=0).reshape(
        pool_count, -1
    )
    wanted = lax.all_to_all(slot_ids, "pool", split_axis=0, concat_axis=0, tiled=True)
    packed = cache_pool[wanted.reshape(-1)].reshape((pool_count, -1) + cache_pool.shape[1:])
    arrived = lax.all_to_all(packed, "pool", split_axis=0, concat_axis=0, tiled=True)
    span = block_table.shape[1] * cache_pool.shape[2]
    blk_len = cache_pool.shape[2]
    entry_of = holder_order.astype(jnp.int32)
    entry_req = entry_of // block_table.shape[1]
    entry_lim = cache_len[entry_req] - (entry_of % block_table.shape[1]) * blk_len
    pos_in_blk = jnp.arange(blk_len, dtype=jnp.int32)
    key_req_c = jnp.where(
        pos_in_blk[None, :] < entry_lim[:, None], entry_req[:, None], -1
    ).reshape(1, -1)
    mp_index = lax.axis_index("mp")
    own_bias = lax.dynamic_slice_in_dim(dense_bias, mp_index * col_width, col_width, 0)
    own_mlp = lax.dynamic_slice_in_dim(mlp_branch, mp_index * col_width, col_width, 1)
    hidden_parts = []
    next_parts = []
    for chunk in range(tok_count // Q_CHUNK):
        rows = slice(chunk * Q_CHUNK, (chunk + 1) * Q_CHUNK)
        attended = attention_call(
            chunk,
            query.reshape(tok_count, col_width),
            arrived,
            key_new.reshape(tok_count, col_width),
            value_new.reshape(tok_count, col_width),
            key_req_c,
            local_req.reshape(1, tok_count),
            local_req.reshape(tok_count, 1),
        )
        partial_out = lax.dot_general(
            attended, w_dense_t, (((1,), (1,)), ((), ())), preferred_element_type=jnp.float32
        )
        pieces = partial_out.astype(jnp.bfloat16).reshape(Q_CHUNK, mp_count, col_width)
        arrived_sums = lax.all_to_all(pieces, "mp", split_axis=1, concat_axis=1, tiled=True)
        dense_total = jnp.sum(arrived_sums.astype(jnp.float32), axis=1)
        hidden_part = (
            residual_in[rows].astype(jnp.float32)
            + dense_total
            + own_bias
            + own_mlp[rows].astype(jnp.float32)
        ).astype(jnp.bfloat16)
        whole_hidden = mp_gather(hidden_part, mp_count)
        normed_next = layer_norm(whole_hidden, next_gain, next_bias).astype(jnp.bfloat16)
        next_raw = jnp.dot(normed_next, w_next_full, preferred_element_type=jnp.float32)
        next_parts.append(
            (next_raw + next_qkv_bias.reshape(1, 3 * col_width))
            .astype(jnp.bfloat16)
            .reshape(Q_CHUNK, 3, col_width)
        )
        hidden_parts.append(hidden_part)
    hidden_out = jnp.concatenate(hidden_parts, axis=0)
    next_qkv = jnp.concatenate(next_parts, axis=0)
    return (hidden_out, next_qkv)


def solution(mesh):
    in_specs = (
        P("pool", "mp"),
        P("pool", None),
        P(),
        P(),
        P("pool", None, "mp"),
        P(None, "mp"),
        P("pool", None, None, "mp"),
        P("mp", "pool"),
        P(),
        P(),
        P(),
        P("pool", None, "mp"),
        P(None, "mp"),
        P("pool"),
        P("pool"),
        P("pool", None),
    )
    out_specs = (P("pool", "mp"), P("pool", None, "mp"))
    return jax.shard_map(local, mesh=mesh, in_specs=in_specs, out_specs=out_specs, check_vma=False)
```

```python
import jax
import jax.numpy as jnp
from jax import lax
from jax.sharding import PartitionSpec as P
from jax.experimental import pallas as pl
from jax.experimental.pallas import tpu as pltpu

HEAD_DIM = 64
ROT = 32


epsilon = 1e-05


def layer_norm(row_data, gain_vec, bias_vec):
    values = row_data.astype(jnp.float32)
    row_mean = jnp.mean(values, axis=-1, keepdims=True)
    centered = values - row_mean
    spread = jnp.mean(centered * centered, axis=-1, keepdims=True)
    return centered * lax.rsqrt(spread + epsilon) * gain_vec + bias_vec


def rotate(head_rows, positions):
    half_rot = ROT // 2
    inverse = 10000.0 ** (-2.0 * jnp.arange(half_rot, dtype=jnp.float32) / ROT)
    angles = positions.astype(jnp.float32)[:, None] * inverse[None, :]
    cosine = jnp.cos(angles)[:, None, :]
    sine = jnp.sin(angles)[:, None, :]
    lower = head_rows[..., :half_rot]
    upper = head_rows[..., half_rot:ROT]
    return jnp.concatenate(
        [lower * cosine - upper * sine, upper * cosine + lower * sine, head_rows[..., ROT:]],
        axis=-1,
    )


def run_starts(token_request):
    tok_total = token_request.shape[0]
    token_index = jnp.arange(tok_total, dtype=jnp.int32)
    change = jnp.concatenate([jnp.ones((1,), dtype=bool), token_request[1:] != token_request[:-1]])
    return (token_index, lax.cummax(jnp.where(change, token_index, 0), axis=0))


def row_folder(left_rows, running, w_piece):
    columns_part = lax.slice_in_dim(left_rows, 0, w_piece.shape[0], axis=1)
    return running + jnp.dot(
        columns_part, w_piece.reshape(w_piece.shape[0], -1), preferred_element_type=jnp.float32
    )


def mp_gather(block, mp_count):
    spread = jnp.broadcast_to(block[None], (mp_count,) + block.shape)
    joined = lax.all_to_all(spread, "mp", split_axis=0, concat_axis=2, tiled=True)
    return joined.reshape(block.shape[0], mp_count * block.shape[1])


def mp_permute_gather(block, mp_count):
    mp_index = lax.axis_index("mp")
    moved = [block] + [
        lax.ppermute(block, "mp", [(src, (src + shift) % mp_count) for src in range(mp_count)])
        for shift in range(1, mp_count)
    ]
    stacked = jnp.stack(moved)
    by_source = stacked[(mp_index - jnp.arange(mp_count)) % mp_count]
    return by_source.transpose(1, 0, 2).reshape(block.shape[0], mp_count * block.shape[1])


Q_CHUNK = 128
PAIR = 128


def attention_body(q_ref, kc_ref, vc_ref, kn_ref, vn_ref, keyc_ref, keyn_ref, qreq_ref, out_ref):
    chunk = pl.program_id(0)
    n_slots = kc_ref.shape[0] * kc_ref.shape[1] * kc_ref.shape[2]
    n_new = kn_ref.shape[0]
    score_scale = HEAD_DIM ** (-0.5)
    q_req = qreq_ref[...]
    mask_c = q_req == keyc_ref[...]
    row_ids = chunk * Q_CHUNK + lax.broadcasted_iota(jnp.int32, (Q_CHUNK, n_new), 0)
    col_ids = lax.broadcasted_iota(jnp.int32, (Q_CHUNK, n_new), 1)
    mask_n = (q_req == keyn_ref[...]) & (col_ids <= row_ids)
    lane = lax.broadcasted_iota(jnp.int32, (1, PAIR), 1)
    nt = (((1,), (1,)), ((), ()))
    for pair in range(out_ref.shape[1] // PAIR):
        cols = slice(pair * PAIR, (pair + 1) * PAIR)
        q_pair = q_ref[:, cols]
        k_pair = kc_ref[:, :, :, cols].reshape(n_slots, PAIR)
        v_pair = vc_ref[:, :, :, cols].reshape(n_slots, PAIR)
        kn_pair = kn_ref[:, cols]
        vn_pair = vn_ref[:, cols]
        halves = []
        for half in range(PAIR // HEAD_DIM):
            in_head = (lane >= half * HEAD_DIM) & (lane < (half + 1) * HEAD_DIM)
            q_head = jnp.where(in_head, q_pair, jnp.zeros_like(q_pair))
            s_c = lax.dot_general(q_head, k_pair, nt, preferred_element_type=jnp.float32)
            s_n = lax.dot_general(q_head, kn_pair, nt, preferred_element_type=jnp.float32)
            s_c = jnp.where(mask_c, s_c * score_scale, -1e30)
            s_n = jnp.where(mask_n, s_n * score_scale, -1e30)
            row_max = jnp.maximum(
                jnp.max(s_c, axis=1, keepdims=True), jnp.max(s_n, axis=1, keepdims=True)
            )
            w_c = jnp.exp(s_c - row_max)
            w_n = jnp.exp(s_n - row_max)
            total = jnp.sum(w_c, axis=1, keepdims=True) + jnp.sum(w_n, axis=1, keepdims=True)
            p_c = (w_c / total).astype(jnp.bfloat16)
            p_n = (w_n / total).astype(jnp.bfloat16)
            o = jnp.dot(p_c, v_pair, preferred_element_type=jnp.float32) + jnp.dot(
                p_n, vn_pair, preferred_element_type=jnp.float32
            )
            halves.append((in_head, o))
        merged = jnp.where(halves[0][0], halves[0][1], halves[1][1])
        out_ref[:, cols] = merged.astype(out_ref.dtype)


def attention_call(query, arrived, key_new, value_new, key_req_c, key_req_n, q_req):
    tok, width = query.shape
    holders, per, _, blk, _ = arrived.shape
    n_slots = holders * per * blk
    grid = (tok // Q_CHUNK,)
    full = lambda c: (0, 0)
    return pl.pallas_call(
        attention_body,
        grid=grid,
        in_specs=[
            pl.BlockSpec((Q_CHUNK, width), lambda c: (c, 0)),
            pl.BlockSpec((holders, per, None, blk, width), lambda c: (0, 0, 0, 0, 0)),
            pl.BlockSpec((holders, per, None, blk, width), lambda c: (0, 0, 1, 0, 0)),
            pl.BlockSpec((tok, width), full),
            pl.BlockSpec((tok, width), full),
            pl.BlockSpec((1, n_slots), full),
            pl.BlockSpec((1, tok), full),
            pl.BlockSpec((Q_CHUNK, 1), lambda c: (c, 0)),
        ],
        out_specs=pl.BlockSpec((Q_CHUNK, width), lambda c: (c, 0)),
        out_shape=jax.ShapeDtypeStruct((tok, width), jnp.bfloat16),
    )(query, arrived, arrived, key_new, value_new, key_req_c, key_req_n, q_req)


def local(
    residual_in,
    mlp_branch,
    norm_gain,
    norm_bias,
    w_qkv,
    qkv_bias,
    cache_pool,
    w_dense,
    dense_bias,
    next_gain,
    next_bias,
    w_next,
    next_qkv_bias,
    token_request,
    cache_len,
    block_table,
):
    mp_count = lax.axis_size("mp")
    full_rows = mp_permute_gather(residual_in, mp_count)
    tok_count = full_rows.shape[0]
    col_width = w_qkv.shape[2]
    head_count = col_width // HEAD_DIM
    normed = layer_norm(full_rows, norm_gain, norm_bias).astype(jnp.bfloat16)
    empty_sum = jnp.zeros((tok_count, 3 * col_width), jnp.float32)
    w_rows = w_qkv.shape[0]
    dense_shard = w_dense.T
    joined = jnp.concatenate(
        [w_qkv.reshape(w_rows, -1), w_next.reshape(w_rows, -1), dense_shard], axis=1
    )
    gathered = lax.all_gather(joined, "pool", axis=0, tiled=True)
    qkv_cols = 3 * col_width
    w_qkv_full = gathered[:, :qkv_cols]
    w_next_full = gathered[:, qkv_cols : 2 * qkv_cols]
    pool_total = lax.axis_size("pool")
    w_dense_t = gathered[:, 2 * qkv_cols :]
    projected = row_folder(normed, empty_sum, w_qkv_full)
    projected = (projected + qkv_bias.reshape(1, 3 * col_width)).reshape(tok_count, 3, col_width)
    token_index, starts = run_starts(token_request)
    request_count = cache_len.shape[0]
    local_req = token_request - request_count * lax.axis_index("pool")
    request_ids = jnp.arange(request_count, dtype=jnp.int32)
    request_match = local_req[:, None] == request_ids[None, :]
    cached_here = jnp.sum(jnp.where(request_match, cache_len[None, :], 0), axis=1)
    positions = cached_here + token_index - starts
    query = rotate(projected[:, 0].reshape(tok_count, head_count, HEAD_DIM), positions).astype(
        jnp.bfloat16
    )
    key_new = rotate(projected[:, 1].reshape(tok_count, head_count, HEAD_DIM), positions).astype(
        jnp.bfloat16
    )
    value_new = projected[:, 2].reshape(tok_count, head_count, HEAD_DIM).astype(jnp.bfloat16)
    pool_count = lax.axis_size("pool")
    blocks_here = cache_pool.shape[0]
    entries = block_table.reshape(-1)
    holder = entries // blocks_here
    entry_ids = jnp.arange(entries.shape[0], dtype=jnp.int32)
    earlier_same = (holder[:, None] == holder[None, :]) & (entry_ids[None, :] < entry_ids[:, None])
    per_holder = entries.shape[0] // pool_count
    slot_of = holder * per_holder + jnp.sum(earlier_same.astype(jnp.int32), axis=1)
    placed = slot_of[:, None] == entry_ids[None, :]
    holder_order = jnp.sum(jnp.where(placed, entry_ids[:, None], 0), axis=0)
    slot_ids = jnp.sum(jnp.where(placed, (entries % blocks_here)[:, None], 0), axis=0).reshape(
        pool_count, -1
    )
    wanted = lax.all_to_all(slot_ids, "pool", split_axis=0, concat_axis=0, tiled=True)
    packed = cache_pool[wanted.reshape(-1)].reshape((pool_count, -1) + cache_pool.shape[1:])
    arrived = lax.all_to_all(packed, "pool", split_axis=0, concat_axis=0, tiled=True)
    span = block_table.shape[1] * cache_pool.shape[2]
    blk_len = cache_pool.shape[2]
    entry_of = holder_order.astype(jnp.int32)
    entry_req = entry_of // block_table.shape[1]
    entry_lim = cache_len[entry_req] - (entry_of % block_table.shape[1]) * blk_len
    pos_in_blk = jnp.arange(blk_len, dtype=jnp.int32)
    key_req_c = jnp.where(
        pos_in_blk[None, :] < entry_lim[:, None], entry_req[:, None], -1
    ).reshape(1, -1)
    attended = attention_call(
        query.reshape(tok_count, col_width),
        arrived,
        key_new.reshape(tok_count, col_width),
        value_new.reshape(tok_count, col_width),
        key_req_c,
        local_req.reshape(1, tok_count),
        local_req.reshape(tok_count, 1),
    )
    partial_out = lax.dot_general(
        attended, w_dense_t, (((1,), (1,)), ((), ())), preferred_element_type=jnp.float32
    )
    mp_index = lax.axis_index("mp")
    pieces = partial_out.astype(jnp.bfloat16).reshape(tok_count, mp_count, col_width)
    arrived_sums = lax.all_to_all(pieces, "mp", split_axis=1, concat_axis=1, tiled=True)
    dense_total = jnp.sum(arrived_sums.astype(jnp.float32), axis=1)
    own_cols = lambda vec: lax.dynamic_slice_in_dim(vec, mp_index * col_width, col_width, 0)
    own_mlp = lax.dynamic_slice_in_dim(mlp_branch, mp_index * col_width, col_width, 1)
    hidden_out = (
        residual_in.astype(jnp.float32)
        + dense_total
        + own_cols(dense_bias)
        + own_mlp.astype(jnp.float32)
    ).astype(jnp.bfloat16)
    whole_hidden = mp_gather(hidden_out, mp_count)
    normed_next = layer_norm(whole_hidden, next_gain, next_bias).astype(jnp.bfloat16)
    next_raw = row_folder(
        normed_next, empty_sum, w_next_full
    )
    next_qkv = (
        (next_raw + next_qkv_bias.reshape(1, 3 * col_width))
        .astype(jnp.bfloat16)
        .reshape(tok_count, 3, col_width)
    )
    return (hidden_out, next_qkv)


def solution(mesh):
    in_specs = (
        P("pool", "mp"),
        P("pool", None),
        P(),
        P(),
        P("pool", None, "mp"),
        P(None, "mp"),
        P("pool", None, None, "mp"),
        P("mp", "pool"),
        P(),
        P(),
        P(),
        P("pool", None, "mp"),
        P(None, "mp"),
        P("pool"),
        P("pool"),
        P("pool", None),
    )
    out_specs = (P("pool", "mp"), P("pool", None, "mp"))
    return jax.shard_map(local, mesh=mesh, in_specs=in_specs, out_specs=out_specs, check_vma=False)
```

```python
import jax
import jax.numpy as jnp
from jax import lax
from jax.sharding import PartitionSpec as P
from jax.experimental import pallas as pl
from jax.experimental.pallas import tpu as pltpu

HEAD_DIM = 64
ROT = 32


epsilon = 1e-05


def layer_norm(row_data, gain_vec, bias_vec):
    values = row_data.astype(jnp.float32)
    row_mean = jnp.mean(values, axis=-1, keepdims=True)
    centered = values - row_mean
    spread = jnp.mean(centered * centered, axis=-1, keepdims=True)
    return centered * lax.rsqrt(spread + epsilon) * gain_vec + bias_vec


def rotate(head_rows, positions):
    half_rot = ROT // 2
    inverse = 10000.0 ** (-2.0 * jnp.arange(half_rot, dtype=jnp.float32) / ROT)
    angles = positions.astype(jnp.float32)[:, None] * inverse[None, :]
    cosine = jnp.cos(angles)[:, None, :]
    sine = jnp.sin(angles)[:, None, :]
    lower = head_rows[..., :half_rot]
    upper = head_rows[..., half_rot:ROT]
    return jnp.concatenate(
        [lower * cosine - upper * sine, upper * cosine + lower * sine, head_rows[..., ROT:]],
        axis=-1,
    )


def run_starts(token_request):
    tok_total = token_request.shape[0]
    token_index = jnp.arange(tok_total, dtype=jnp.int32)
    change = jnp.concatenate([jnp.ones((1,), dtype=bool), token_request[1:] != token_request[:-1]])
    return (token_index, lax.cummax(jnp.where(change, token_index, 0), axis=0))


def row_folder(left_rows, running, w_piece):
    columns_part = lax.slice_in_dim(left_rows, 0, w_piece.shape[0], axis=1)
    return running + jnp.dot(
        columns_part, w_piece.reshape(w_piece.shape[0], -1), preferred_element_type=jnp.float32
    )


def mp_gather(block, mp_count):
    spread = jnp.broadcast_to(block[None], (mp_count,) + block.shape)
    joined = lax.all_to_all(spread, "mp", split_axis=0, concat_axis=2, tiled=True)
    return joined.reshape(block.shape[0], mp_count * block.shape[1])


def mp_permute_gather(block, mp_count):
    mp_index = lax.axis_index("mp")
    moved = [block] + [
        lax.ppermute(block, "mp", [(src, (src + shift) % mp_count) for src in range(mp_count)])
        for shift in range(1, mp_count)
    ]
    stacked = jnp.stack(moved)
    by_source = stacked[(mp_index - jnp.arange(mp_count)) % mp_count]
    return by_source.transpose(1, 0, 2).reshape(block.shape[0], mp_count * block.shape[1])


Q_CHUNK = 128
PAIR = 128


def attention_body(q_ref, kc_ref, vc_ref, kn_ref, vn_ref, keyc_ref, keyn_ref, qreq_ref, out_ref):
    chunk = pl.program_id(0)
    n_slots = kc_ref.shape[0] * kc_ref.shape[1] * kc_ref.shape[2]
    n_new = kn_ref.shape[0]
    score_scale = HEAD_DIM ** (-0.5)
    q_req = qreq_ref[...]
    mask_c = q_req == keyc_ref[...]
    row_ids = chunk * Q_CHUNK + lax.broadcasted_iota(jnp.int32, (Q_CHUNK, n_new), 0)
    col_ids = lax.broadcasted_iota(jnp.int32, (Q_CHUNK, n_new), 1)
    mask_n = (q_req == keyn_ref[...]) & (col_ids <= row_ids)
    lane = lax.broadcasted_iota(jnp.int32, (1, PAIR), 1)
    nt = (((1,), (1,)), ((), ()))
    for pair in range(out_ref.shape[1] // PAIR):
        cols = slice(pair * PAIR, (pair + 1) * PAIR)
        q_pair = q_ref[:, cols]
        k_pair = kc_ref[:, :, :, cols].reshape(n_slots, PAIR)
        v_pair = vc_ref[:, :, :, cols].reshape(n_slots, PAIR)
        kn_pair = kn_ref[:, cols]
        vn_pair = vn_ref[:, cols]
        halves = []
        for half in range(PAIR // HEAD_DIM):
            in_head = (lane >= half * HEAD_DIM) & (lane < (half + 1) * HEAD_DIM)
            q_head = jnp.where(in_head, q_pair, jnp.zeros_like(q_pair))
            s_c = lax.dot_general(q_head, k_pair, nt, preferred_element_type=jnp.float32)
            s_n = lax.dot_general(q_head, kn_pair, nt, preferred_element_type=jnp.float32)
            s_c = jnp.where(mask_c, s_c * score_scale, -1e30)
            s_n = jnp.where(mask_n, s_n * score_scale, -1e30)
            row_max = jnp.maximum(
                jnp.max(s_c, axis=1, keepdims=True), jnp.max(s_n, axis=1, keepdims=True)
            )
            w_c = jnp.exp(s_c - row_max)
            w_n = jnp.exp(s_n - row_max)
            total = jnp.sum(w_c, axis=1, keepdims=True) + jnp.sum(w_n, axis=1, keepdims=True)
            p_c = (w_c / total).astype(jnp.bfloat16)
            p_n = (w_n / total).astype(jnp.bfloat16)
            o = jnp.dot(p_c, v_pair, preferred_element_type=jnp.float32) + jnp.dot(
                p_n, vn_pair, preferred_element_type=jnp.float32
            )
            halves.append((in_head, o))
        merged = jnp.where(halves[0][0], halves[0][1], halves[1][1])
        out_ref[:, cols] = merged.astype(out_ref.dtype)


def attention_call(query, arrived, key_new, value_new, key_req_c, key_req_n, q_req):
    tok, width = query.shape
    holders, per, _, blk, _ = arrived.shape
    n_slots = holders * per * blk
    grid = (tok // Q_CHUNK,)
    full = lambda c: (0, 0)
    return pl.pallas_call(
        attention_body,
        grid=grid,
        in_specs=[
            pl.BlockSpec((Q_CHUNK, width), lambda c: (c, 0)),
            pl.BlockSpec((holders, per, None, blk, width), lambda c: (0, 0, 0, 0, 0)),
            pl.BlockSpec((holders, per, None, blk, width), lambda c: (0, 0, 1, 0, 0)),
            pl.BlockSpec((tok, width), full),
            pl.BlockSpec((tok, width), full),
            pl.BlockSpec((1, n_slots), full),
            pl.BlockSpec((1, tok), full),
            pl.BlockSpec((Q_CHUNK, 1), lambda c: (c, 0)),
        ],
        out_specs=pl.BlockSpec((Q_CHUNK, width), lambda c: (c, 0)),
        out_shape=jax.ShapeDtypeStruct((tok, width), jnp.bfloat16),
    )(query, arrived, arrived, key_new, value_new, key_req_c, key_req_n, q_req)


def local(
    residual_in,
    mlp_branch,
    norm_gain,
    norm_bias,
    w_qkv,
    qkv_bias,
    cache_pool,
    w_dense,
    dense_bias,
    next_gain,
    next_bias,
    w_next,
    next_qkv_bias,
    token_request,
    cache_len,
    block_table,
):
    mp_count = lax.axis_size("mp")
    full_rows = mp_permute_gather(residual_in, mp_count)
    tok_count = full_rows.shape[0]
    col_width = w_qkv.shape[2]
    head_count = col_width // HEAD_DIM
    normed = layer_norm(full_rows, norm_gain, norm_bias).astype(jnp.bfloat16)
    empty_sum = jnp.zeros((tok_count, 3 * col_width), jnp.float32)
    w_rows = w_qkv.shape[0]
    dense_shard = w_dense.T
    joined = jnp.concatenate(
        [w_qkv.reshape(w_rows, -1), w_next.reshape(w_rows, -1), dense_shard], axis=1
    )
    gathered = lax.all_gather(joined, "pool", axis=0, tiled=True)
    qkv_cols = 3 * col_width
    w_qkv_full = gathered[:, :qkv_cols]
    w_next_full = gathered[:, qkv_cols : 2 * qkv_cols]
    pool_total = lax.axis_size("pool")
    w_dense_t = gathered[:, 2 * qkv_cols :]
    projected = row_folder(normed, empty_sum, w_qkv_full)
    projected = (projected + qkv_bias.reshape(1, 3 * col_width)).reshape(tok_count, 3, col_width)
    token_index, starts = run_starts(token_request)
    request_count = cache_len.shape[0]
    local_req = token_request - request_count * lax.axis_index("pool")
    request_ids = jnp.arange(request_count, dtype=jnp.int32)
    request_match = local_req[:, None] == request_ids[None, :]
    cached_here = jnp.sum(jnp.where(request_match, cache_len[None, :], 0), axis=1)
    positions = cached_here + token_index - starts
    query = rotate(projected[:, 0].reshape(tok_count, head_count, HEAD_DIM), positions).astype(
        jnp.bfloat16
    )
    key_new = rotate(projected[:, 1].reshape(tok_count, head_count, HEAD_DIM), positions).astype(
        jnp.bfloat16
    )
    value_new = projected[:, 2].reshape(tok_count, head_count, HEAD_DIM).astype(jnp.bfloat16)
    pool_count = lax.axis_size("pool")
    blocks_here = cache_pool.shape[0]
    entries = block_table.reshape(-1)
    holder = entries // blocks_here
    entry_ids = jnp.arange(entries.shape[0], dtype=jnp.int32)
    earlier_same = (holder[:, None] == holder[None, :]) & (entry_ids[None, :] < entry_ids[:, None])
    per_holder = entries.shape[0] // pool_count
    slot_of = holder * per_holder + jnp.sum(earlier_same.astype(jnp.int32), axis=1)
    placed = slot_of[:, None] == entry_ids[None, :]
    holder_order = jnp.sum(jnp.where(placed, entry_ids[:, None], 0), axis=0)
    slot_ids = jnp.sum(jnp.where(placed, (entries % blocks_here)[:, None], 0), axis=0).reshape(
        pool_count, -1
    )
    wanted = lax.all_to_all(slot_ids, "pool", split_axis=0, concat_axis=0, tiled=True)
    packed = cache_pool[wanted.reshape(-1)].reshape((pool_count, -1) + cache_pool.shape[1:])
    arrived = lax.all_to_all(packed, "pool", split_axis=0, concat_axis=0, tiled=True)
    span = block_table.shape[1] * cache_pool.shape[2]
    blk_len = cache_pool.shape[2]
    entry_of = holder_order.astype(jnp.int32)
    entry_req = entry_of // block_table.shape[1]
    entry_lim = cache_len[entry_req] - (entry_of % block_table.shape[1]) * blk_len
    pos_in_blk = jnp.arange(blk_len, dtype=jnp.int32)
    key_req_c = jnp.where(
        pos_in_blk[None, :] < entry_lim[:, None], entry_req[:, None], -1
    ).reshape(1, -1)
    attended = attention_call(
        query.reshape(tok_count, col_width),
        arrived,
        key_new.reshape(tok_count, col_width),
        value_new.reshape(tok_count, col_width),
        key_req_c,
        local_req.reshape(1, tok_count),
        local_req.reshape(tok_count, 1),
    )
    partial_out = jnp.einsum(
        "tr,jcr->jtc",
        attended,
        w_dense_t.reshape(mp_count, col_width, -1),
        preferred_element_type=jnp.float32,
    )
    mp_index = lax.axis_index("mp")
    pieces = partial_out.astype(jnp.bfloat16)
    arrived_sums = lax.all_to_all(pieces, "mp", split_axis=0, concat_axis=0, tiled=True)
    dense_total = jnp.sum(arrived_sums.astype(jnp.float32), axis=0)
    own_cols = lambda vec: lax.dynamic_slice_in_dim(vec, mp_index * col_width, col_width, 0)
    own_mlp = lax.dynamic_slice_in_dim(mlp_branch, mp_index * col_width, col_width, 1)
    hidden_out = (
        residual_in.astype(jnp.float32)
        + dense_total
        + own_cols(dense_bias)
        + own_mlp.astype(jnp.float32)
    ).astype(jnp.bfloat16)
    whole_hidden = mp_gather(hidden_out, mp_count)
    normed_next = layer_norm(whole_hidden, next_gain, next_bias).astype(jnp.bfloat16)
    next_raw = row_folder(
        normed_next, empty_sum, w_next_full
    )
    next_qkv = (
        (next_raw + next_qkv_bias.reshape(1, 3 * col_width))
        .astype(jnp.bfloat16)
        .reshape(tok_count, 3, col_width)
    )
    return (hidden_out, next_qkv)


def solution(mesh):
    in_specs = (
        P("pool", "mp"),
        P("pool", None),
        P(),
        P(),
        P("pool", None, "mp"),
        P(None, "mp"),
        P("pool", None, None, "mp"),
        P("mp", "pool"),
        P(),
        P(),
        P(),
        P("pool", None, "mp"),
        P(None, "mp"),
        P("pool"),
        P("pool"),
        P("pool", None),
    )
    out_specs = (P("pool", "mp"), P("pool", None, "mp"))
    return jax.shard_map(local, mesh=mesh, in_specs=in_specs, out_specs=out_specs, check_vma=False)
```

```python
import jax
import jax.numpy as jnp
from jax import lax
from jax.sharding import PartitionSpec as P
from jax.experimental import pallas as pl
from jax.experimental.pallas import tpu as pltpu

HEAD_DIM = 64
ROT = 32


epsilon = 1e-05


def layer_norm(row_data, gain_vec, bias_vec):
    values = row_data.astype(jnp.float32)
    row_mean = jnp.mean(values, axis=-1, keepdims=True)
    centered = values - row_mean
    spread = jnp.mean(centered * centered, axis=-1, keepdims=True)
    return centered * lax.rsqrt(spread + epsilon) * gain_vec + bias_vec


def rotate(head_rows, positions):
    half_rot = ROT // 2
    inverse = 10000.0 ** (-2.0 * jnp.arange(half_rot, dtype=jnp.float32) / ROT)
    angles = positions.astype(jnp.float32)[:, None] * inverse[None, :]
    cosine = jnp.cos(angles)[:, None, :]
    sine = jnp.sin(angles)[:, None, :]
    lower = head_rows[..., :half_rot]
    upper = head_rows[..., half_rot:ROT]
    return jnp.concatenate(
        [lower * cosine - upper * sine, upper * cosine + lower * sine, head_rows[..., ROT:]],
        axis=-1,
    )


def run_starts(token_request):
    tok_total = token_request.shape[0]
    token_index = jnp.arange(tok_total, dtype=jnp.int32)
    change = jnp.concatenate([jnp.ones((1,), dtype=bool), token_request[1:] != token_request[:-1]])
    return (token_index, lax.cummax(jnp.where(change, token_index, 0), axis=0))


def row_folder(left_rows, running, w_piece):
    columns_part = lax.slice_in_dim(left_rows, 0, w_piece.shape[0], axis=1)
    return running + jnp.dot(
        columns_part, w_piece.reshape(w_piece.shape[0], -1), preferred_element_type=jnp.float32
    )


def mp_gather(block, mp_count):
    spread = jnp.broadcast_to(block[None], (mp_count,) + block.shape)
    joined = lax.all_to_all(spread, "mp", split_axis=0, concat_axis=2, tiled=True)
    return joined.reshape(block.shape[0], mp_count * block.shape[1])


def mp_permute_gather(block, mp_count):
    mp_index = lax.axis_index("mp")
    moved = [block] + [
        lax.ppermute(block, "mp", [(src, (src + shift) % mp_count) for src in range(mp_count)])
        for shift in range(1, mp_count)
    ]
    stacked = jnp.stack(moved)
    by_source = stacked[(mp_index - jnp.arange(mp_count)) % mp_count]
    return by_source.transpose(1, 0, 2).reshape(block.shape[0], mp_count * block.shape[1])


Q_CHUNK = 128
PAIR = 128


def attention_body(q_ref, kc_ref, vc_ref, kn_ref, vn_ref, keyc_ref, keyn_ref, qreq_ref, out_ref):
    chunk = pl.program_id(1)
    n_slots = kc_ref.shape[0] * kc_ref.shape[1] * kc_ref.shape[2]
    n_new = kn_ref.shape[0]
    score_scale = HEAD_DIM ** (-0.5)
    q_req = qreq_ref[...]
    mask_c = q_req == keyc_ref[...]
    row_ids = chunk * Q_CHUNK + lax.broadcasted_iota(jnp.int32, (Q_CHUNK, n_new), 0)
    col_ids = lax.broadcasted_iota(jnp.int32, (Q_CHUNK, n_new), 1)
    mask_n = (q_req == keyn_ref[...]) & (col_ids <= row_ids)
    lane = lax.broadcasted_iota(jnp.int32, (1, PAIR), 1)
    nt = (((1,), (1,)), ((), ()))
    q_pair = q_ref[...]
    k_pair = kc_ref[...].reshape(n_slots, PAIR)
    v_pair = vc_ref[...].reshape(n_slots, PAIR)
    kn_pair = kn_ref[...]
    vn_pair = vn_ref[...]
    halves = []
    for half in range(PAIR // HEAD_DIM):
        in_head = (lane >= half * HEAD_DIM) & (lane < (half + 1) * HEAD_DIM)
        q_head = jnp.where(in_head, q_pair, jnp.zeros_like(q_pair))
        s_c = lax.dot_general(q_head, k_pair, nt, preferred_element_type=jnp.float32)
        s_n = lax.dot_general(q_head, kn_pair, nt, preferred_element_type=jnp.float32)
        s_c = jnp.where(mask_c, s_c * score_scale, -1e30)
        s_n = jnp.where(mask_n, s_n * score_scale, -1e30)
        row_max = jnp.maximum(
            jnp.max(s_c, axis=1, keepdims=True), jnp.max(s_n, axis=1, keepdims=True)
        )
        w_c = jnp.exp(s_c - row_max)
        w_n = jnp.exp(s_n - row_max)
        total = jnp.sum(w_c, axis=1, keepdims=True) + jnp.sum(w_n, axis=1, keepdims=True)
        p_c = (w_c / total).astype(jnp.bfloat16)
        p_n = (w_n / total).astype(jnp.bfloat16)
        o = jnp.dot(p_c, v_pair, preferred_element_type=jnp.float32) + jnp.dot(
            p_n, vn_pair, preferred_element_type=jnp.float32
        )
        halves.append((in_head, o))
    merged = jnp.where(halves[0][0], halves[0][1], halves[1][1])
    out_ref[...] = merged.astype(out_ref.dtype)


def attention_call(query, arrived, key_new, value_new, key_req_c, key_req_n, q_req):
    tok, width = query.shape
    holders, per, _, blk, _ = arrived.shape
    n_slots = holders * per * blk
    grid = (width // PAIR, tok // Q_CHUNK)
    full = lambda p, c: (0, 0)
    return pl.pallas_call(
        attention_body,
        grid=grid,
        in_specs=[
            pl.BlockSpec((Q_CHUNK, PAIR), lambda p, c: (c, p)),
            pl.BlockSpec((holders, per, None, blk, PAIR), lambda p, c: (0, 0, 0, 0, p)),
            pl.BlockSpec((holders, per, None, blk, PAIR), lambda p, c: (0, 0, 1, 0, p)),
            pl.BlockSpec((tok, PAIR), lambda p, c: (0, p)),
            pl.BlockSpec((tok, PAIR), lambda p, c: (0, p)),
            pl.BlockSpec((1, n_slots), full),
            pl.BlockSpec((1, tok), full),
            pl.BlockSpec((Q_CHUNK, 1), lambda p, c: (c, 0)),
        ],
        out_specs=pl.BlockSpec((Q_CHUNK, PAIR), lambda p, c: (c, p)),
        out_shape=jax.ShapeDtypeStruct((tok, width), jnp.bfloat16),
    )(query, arrived, arrived, key_new, value_new, key_req_c, key_req_n, q_req)


def local(
    residual_in,
    mlp_branch,
    norm_gain,
    norm_bias,
    w_qkv,
    qkv_bias,
    cache_pool,
    w_dense,
    dense_bias,
    next_gain,
    next_bias,
    w_next,
    next_qkv_bias,
    token_request,
    cache_len,
    block_table,
):
    mp_count = lax.axis_size("mp")
    full_rows = mp_permute_gather(residual_in, mp_count)
    tok_count = full_rows.shape[0]
    col_width = w_qkv.shape[2]
    head_count = col_width // HEAD_DIM
    normed = layer_norm(full_rows, norm_gain, norm_bias).astype(jnp.bfloat16)
    empty_sum = jnp.zeros((tok_count, 3 * col_width), jnp.float32)
    w_rows = w_qkv.shape[0]
    dense_shard = w_dense.T
    joined = jnp.concatenate(
        [w_qkv.reshape(w_rows, -1), w_next.reshape(w_rows, -1), dense_shard], axis=1
    )
    gathered = lax.all_gather(joined, "pool", axis=0, tiled=True)
    qkv_cols = 3 * col_width
    w_qkv_full = gathered[:, :qkv_cols]
    w_next_full = gathered[:, qkv_cols : 2 * qkv_cols]
    pool_total = lax.axis_size("pool")
    w_dense_t = gathered[:, 2 * qkv_cols :]
    projected = row_folder(normed, empty_sum, w_qkv_full)
    projected = (projected + qkv_bias.reshape(1, 3 * col_width)).reshape(tok_count, 3, col_width)
    token_index, starts = run_starts(token_request)
    request_count = cache_len.shape[0]
    local_req = token_request - request_count * lax.axis_index("pool")
    request_ids = jnp.arange(request_count, dtype=jnp.int32)
    request_match = local_req[:, None] == request_ids[None, :]
    cached_here = jnp.sum(jnp.where(request_match, cache_len[None, :], 0), axis=1)
    positions = cached_here + token_index - starts
    query = rotate(projected[:, 0].reshape(tok_count, head_count, HEAD_DIM), positions).astype(
        jnp.bfloat16
    )
    key_new = rotate(projected[:, 1].reshape(tok_count, head_count, HEAD_DIM), positions).astype(
        jnp.bfloat16
    )
    value_new = projected[:, 2].reshape(tok_count, head_count, HEAD_DIM).astype(jnp.bfloat16)
    pool_count = lax.axis_size("pool")
    blocks_here = cache_pool.shape[0]
    entries = block_table.reshape(-1)
    holder = entries // blocks_here
    entry_ids = jnp.arange(entries.shape[0], dtype=jnp.int32)
    earlier_same = (holder[:, None] == holder[None, :]) & (entry_ids[None, :] < entry_ids[:, None])
    per_holder = entries.shape[0] // pool_count
    slot_of = holder * per_holder + jnp.sum(earlier_same.astype(jnp.int32), axis=1)
    placed = slot_of[:, None] == entry_ids[None, :]
    holder_order = jnp.sum(jnp.where(placed, entry_ids[:, None], 0), axis=0)
    slot_ids = jnp.sum(jnp.where(placed, (entries % blocks_here)[:, None], 0), axis=0).reshape(
        pool_count, -1
    )
    wanted = lax.all_to_all(slot_ids, "pool", split_axis=0, concat_axis=0, tiled=True)
    packed = cache_pool[wanted.reshape(-1)].reshape((pool_count, -1) + cache_pool.shape[1:])
    arrived = lax.all_to_all(packed, "pool", split_axis=0, concat_axis=0, tiled=True)
    span = block_table.shape[1] * cache_pool.shape[2]
    blk_len = cache_pool.shape[2]
    entry_of = holder_order.astype(jnp.int32)
    entry_req = entry_of // block_table.shape[1]
    entry_lim = cache_len[entry_req] - (entry_of % block_table.shape[1]) * blk_len
    pos_in_blk = jnp.arange(blk_len, dtype=jnp.int32)
    key_req_c = jnp.where(
        pos_in_blk[None, :] < entry_lim[:, None], entry_req[:, None], -1
    ).reshape(1, -1)
    attended = attention_call(
        query.reshape(tok_count, col_width),
        arrived,
        key_new.reshape(tok_count, col_width),
        value_new.reshape(tok_count, col_width),
        key_req_c,
        local_req.reshape(1, tok_count),
        local_req.reshape(tok_count, 1),
    )
    partial_out = lax.dot_general(
        attended, w_dense_t, (((1,), (1,)), ((), ())), preferred_element_type=jnp.float32
    )
    mp_index = lax.axis_index("mp")
    pieces = partial_out.astype(jnp.bfloat16).reshape(tok_count, mp_count, col_width)
    arrived_sums = lax.all_to_all(pieces, "mp", split_axis=1, concat_axis=1, tiled=True)
    dense_total = jnp.sum(arrived_sums.astype(jnp.float32), axis=1)
    own_cols = lambda vec: lax.dynamic_slice_in_dim(vec, mp_index * col_width, col_width, 0)
    own_mlp = lax.dynamic_slice_in_dim(mlp_branch, mp_index * col_width, col_width, 1)
    hidden_out = (
        residual_in.astype(jnp.float32)
        + dense_total
        + own_cols(dense_bias)
        + own_mlp.astype(jnp.float32)
    ).astype(jnp.bfloat16)
    whole_hidden = mp_gather(hidden_out, mp_count)
    normed_next = layer_norm(whole_hidden, next_gain, next_bias).astype(jnp.bfloat16)
    next_raw = row_folder(
        normed_next, empty_sum, w_next_full
    )
    next_qkv = (
        (next_raw + next_qkv_bias.reshape(1, 3 * col_width))
        .astype(jnp.bfloat16)
        .reshape(tok_count, 3, col_width)
    )
    return (hidden_out, next_qkv)


def solution(mesh):
    in_specs = (
        P("pool", "mp"),
        P("pool", None),
        P(),
        P(),
        P("pool", None, "mp"),
        P(None, "mp"),
        P("pool", None, None, "mp"),
        P("mp", "pool"),
        P(),
        P(),
        P(),
        P("pool", None, "mp"),
        P(None, "mp"),
        P("pool"),
        P("pool"),
        P("pool", None),
    )
    out_specs = (P("pool", "mp"), P("pool", None, "mp"))
    return jax.shard_map(local, mesh=mesh, in_specs=in_specs, out_specs=out_specs, check_vma=False)
```

```python
import jax
import jax.numpy as jnp
from jax import lax
from jax.sharding import PartitionSpec as P
from jax.experimental import pallas as pl
from jax.experimental.pallas import tpu as pltpu

HEAD_DIM = 64
ROT = 32


epsilon = 1e-05


def layer_norm(row_data, gain_vec, bias_vec):
    values = row_data.astype(jnp.float32)
    row_mean = jnp.mean(values, axis=-1, keepdims=True)
    centered = values - row_mean
    spread = jnp.mean(centered * centered, axis=-1, keepdims=True)
    return centered * lax.rsqrt(spread + epsilon) * gain_vec + bias_vec


def rotate(head_rows, positions):
    half_rot = ROT // 2
    inverse = 10000.0 ** (-2.0 * jnp.arange(half_rot, dtype=jnp.float32) / ROT)
    angles = positions.astype(jnp.float32)[:, None] * inverse[None, :]
    cosine = jnp.cos(angles)[:, None, :]
    sine = jnp.sin(angles)[:, None, :]
    lower = head_rows[..., :half_rot]
    upper = head_rows[..., half_rot:ROT]
    return jnp.concatenate(
        [lower * cosine - upper * sine, upper * cosine + lower * sine, head_rows[..., ROT:]],
        axis=-1,
    )


def run_starts(token_request):
    tok_total = token_request.shape[0]
    token_index = jnp.arange(tok_total, dtype=jnp.int32)
    change = jnp.concatenate([jnp.ones((1,), dtype=bool), token_request[1:] != token_request[:-1]])
    return (token_index, lax.cummax(jnp.where(change, token_index, 0), axis=0))


def row_folder(left_rows, running, w_piece):
    columns_part = lax.slice_in_dim(left_rows, 0, w_piece.shape[0], axis=1)
    return running + jnp.dot(
        columns_part, w_piece.reshape(w_piece.shape[0], -1), preferred_element_type=jnp.float32
    )


def mp_gather(block, mp_count):
    spread = jnp.broadcast_to(block[None], (mp_count,) + block.shape)
    joined = lax.all_to_all(spread, "mp", split_axis=0, concat_axis=2, tiled=True)
    return joined.reshape(block.shape[0], mp_count * block.shape[1])


def mp_permute_gather(block, mp_count):
    mp_index = lax.axis_index("mp")
    moved = [block] + [
        lax.ppermute(block, "mp", [(src, (src + shift) % mp_count) for src in range(mp_count)])
        for shift in range(1, mp_count)
    ]
    stacked = jnp.stack(moved)
    by_source = stacked[(mp_index - jnp.arange(mp_count)) % mp_count]
    return by_source.transpose(1, 0, 2).reshape(block.shape[0], mp_count * block.shape[1])


Q_CHUNK = 128
PAIR = 128


def attention_body(q_ref, kc_ref, vc_ref, kn_ref, vn_ref, keyc_ref, keyn_ref, qreq_ref, out_ref):
    chunk = pl.program_id(1)
    n_slots = kc_ref.shape[0] * kc_ref.shape[1] * kc_ref.shape[2]
    n_new = kn_ref.shape[0]
    score_scale = HEAD_DIM ** (-0.5)
    q_req = qreq_ref[...]
    mask_c = q_req == keyc_ref[...]
    row_ids = chunk * Q_CHUNK + lax.broadcasted_iota(jnp.int32, (Q_CHUNK, n_new), 0)
    col_ids = lax.broadcasted_iota(jnp.int32, (Q_CHUNK, n_new), 1)
    mask_n = (q_req == keyn_ref[...]) & (col_ids <= row_ids)
    lane = lax.broadcasted_iota(jnp.int32, (1, PAIR), 1)
    nt = (((1,), (1,)), ((), ()))
    q_pair = q_ref[...]
    k_pair = kc_ref[...].reshape(n_slots, PAIR)
    v_pair = vc_ref[...].reshape(n_slots, PAIR)
    kn_pair = kn_ref[...]
    vn_pair = vn_ref[...]
    halves = []
    for half in range(PAIR // HEAD_DIM):
        in_head = (lane >= half * HEAD_DIM) & (lane < (half + 1) * HEAD_DIM)
        q_head = jnp.where(in_head, q_pair * jnp.asarray(score_scale, q_pair.dtype), jnp.zeros_like(q_pair))
        s_c = lax.dot_general(q_head, k_pair, nt, preferred_element_type=jnp.float32)
        s_n = lax.dot_general(q_head, kn_pair, nt, preferred_element_type=jnp.float32)
        s_c = jnp.where(mask_c, s_c, -1e30)
        s_n = jnp.where(mask_n, s_n, -1e30)
        row_max = jnp.maximum(
            jnp.max(s_c, axis=1, keepdims=True), jnp.max(s_n, axis=1, keepdims=True)
        )
        w_c = jnp.exp(s_c - row_max)
        w_n = jnp.exp(s_n - row_max)
        total = jnp.sum(w_c, axis=1, keepdims=True) + jnp.sum(w_n, axis=1, keepdims=True)
        inv_total = 1.0 / total
        p_c = (w_c * inv_total).astype(jnp.bfloat16)
        p_n = (w_n * inv_total).astype(jnp.bfloat16)
        o = jnp.dot(p_c, v_pair, preferred_element_type=jnp.float32) + jnp.dot(
            p_n, vn_pair, preferred_element_type=jnp.float32
        )
        halves.append((in_head, o))
    merged = jnp.where(halves[0][0], halves[0][1], halves[1][1])
    out_ref[...] = merged.astype(out_ref.dtype)


def attention_call(query, arrived, key_new, value_new, key_req_c, key_req_n, q_req):
    tok, width = query.shape
    holders, per, _, blk, _ = arrived.shape
    n_slots = holders * per * blk
    grid = (width // PAIR, tok // Q_CHUNK)
    full = lambda p, c: (0, 0)
    return pl.pallas_call(
        attention_body,
        grid=grid,
        in_specs=[
            pl.BlockSpec((Q_CHUNK, PAIR), lambda p, c: (c, p)),
            pl.BlockSpec((holders, per, None, blk, PAIR), lambda p, c: (0, 0, 0, 0, p)),
            pl.BlockSpec((holders, per, None, blk, PAIR), lambda p, c: (0, 0, 1, 0, p)),
            pl.BlockSpec((tok, PAIR), lambda p, c: (0, p)),
            pl.BlockSpec((tok, PAIR), lambda p, c: (0, p)),
            pl.BlockSpec((1, n_slots), full),
            pl.BlockSpec((1, tok), full),
            pl.BlockSpec((Q_CHUNK, 1), lambda p, c: (c, 0)),
        ],
        out_specs=pl.BlockSpec((Q_CHUNK, PAIR), lambda p, c: (c, p)),
        out_shape=jax.ShapeDtypeStruct((tok, width), jnp.bfloat16),
    )(query, arrived, arrived, key_new, value_new, key_req_c, key_req_n, q_req)


def local(
    residual_in,
    mlp_branch,
    norm_gain,
    norm_bias,
    w_qkv,
    qkv_bias,
    cache_pool,
    w_dense,
    dense_bias,
    next_gain,
    next_bias,
    w_next,
    next_qkv_bias,
    token_request,
    cache_len,
    block_table,
):
    mp_count = lax.axis_size("mp")
    full_rows = mp_permute_gather(residual_in, mp_count)
    tok_count = full_rows.shape[0]
    col_width = w_qkv.shape[2]
    head_count = col_width // HEAD_DIM
    normed = layer_norm(full_rows, norm_gain, norm_bias).astype(jnp.bfloat16)
    empty_sum = jnp.zeros((tok_count, 3 * col_width), jnp.float32)
    w_rows = w_qkv.shape[0]
    dense_shard = w_dense.T
    joined = jnp.concatenate(
        [w_qkv.reshape(w_rows, -1), w_next.reshape(w_rows, -1), dense_shard], axis=1
    )
    gathered = lax.all_gather(joined, "pool", axis=0, tiled=True)
    qkv_cols = 3 * col_width
    w_qkv_full = gathered[:, :qkv_cols]
    w_next_full = gathered[:, qkv_cols : 2 * qkv_cols]
    pool_total = lax.axis_size("pool")
    w_dense_t = gathered[:, 2 * qkv_cols :]
    projected = row_folder(normed, empty_sum, w_qkv_full)
    projected = (projected + qkv_bias.reshape(1, 3 * col_width)).reshape(tok_count, 3, col_width)
    token_index, starts = run_starts(token_request)
    request_count = cache_len.shape[0]
    local_req = token_request - request_count * lax.axis_index("pool")
    request_ids = jnp.arange(request_count, dtype=jnp.int32)
    request_match = local_req[:, None] == request_ids[None, :]
    cached_here = jnp.sum(jnp.where(request_match, cache_len[None, :], 0), axis=1)
    positions = cached_here + token_index - starts
    query = rotate(projected[:, 0].reshape(tok_count, head_count, HEAD_DIM), positions).astype(
        jnp.bfloat16
    )
    key_new = rotate(projected[:, 1].reshape(tok_count, head_count, HEAD_DIM), positions).astype(
        jnp.bfloat16
    )
    value_new = projected[:, 2].reshape(tok_count, head_count, HEAD_DIM).astype(jnp.bfloat16)
    pool_count = lax.axis_size("pool")
    blocks_here = cache_pool.shape[0]
    entries = block_table.reshape(-1)
    holder = entries // blocks_here
    entry_ids = jnp.arange(entries.shape[0], dtype=jnp.int32)
    earlier_same = (holder[:, None] == holder[None, :]) & (entry_ids[None, :] < entry_ids[:, None])
    per_holder = entries.shape[0] // pool_count
    slot_of = holder * per_holder + jnp.sum(earlier_same.astype(jnp.int32), axis=1)
    placed = slot_of[:, None] == entry_ids[None, :]
    holder_order = jnp.sum(jnp.where(placed, entry_ids[:, None], 0), axis=0)
    slot_ids = jnp.sum(jnp.where(placed, (entries % blocks_here)[:, None], 0), axis=0).reshape(
        pool_count, -1
    )
    wanted = lax.all_to_all(slot_ids, "pool", split_axis=0, concat_axis=0, tiled=True)
    packed = cache_pool[wanted.reshape(-1)].reshape((pool_count, -1) + cache_pool.shape[1:])
    arrived = lax.all_to_all(packed, "pool", split_axis=0, concat_axis=0, tiled=True)
    span = block_table.shape[1] * cache_pool.shape[2]
    blk_len = cache_pool.shape[2]
    entry_of = holder_order.astype(jnp.int32)
    entry_req = entry_of // block_table.shape[1]
    entry_lim = cache_len[entry_req] - (entry_of % block_table.shape[1]) * blk_len
    pos_in_blk = jnp.arange(blk_len, dtype=jnp.int32)
    key_req_c = jnp.where(
        pos_in_blk[None, :] < entry_lim[:, None], entry_req[:, None], -1
    ).reshape(1, -1)
    attended = attention_call(
        query.reshape(tok_count, col_width),
        arrived,
        key_new.reshape(tok_count, col_width),
        value_new.reshape(tok_count, col_width),
        key_req_c,
        local_req.reshape(1, tok_count),
        local_req.reshape(tok_count, 1),
    )
    partial_out = lax.dot_general(
        attended, w_dense_t, (((1,), (1,)), ((), ())), preferred_element_type=jnp.float32
    )
    mp_index = lax.axis_index("mp")
    pieces = partial_out.astype(jnp.bfloat16).reshape(tok_count, mp_count, col_width)
    arrived_sums = lax.all_to_all(pieces, "mp", split_axis=1, concat_axis=1, tiled=True)
    dense_total = jnp.sum(arrived_sums.astype(jnp.float32), axis=1)
    own_cols = lambda vec: lax.dynamic_slice_in_dim(vec, mp_index * col_width, col_width, 0)
    own_mlp = lax.dynamic_slice_in_dim(mlp_branch, mp_index * col_width, col_width, 1)
    hidden_out = (
        residual_in.astype(jnp.float32)
        + dense_total
        + own_cols(dense_bias)
        + own_mlp.astype(jnp.float32)
    ).astype(jnp.bfloat16)
    whole_hidden = mp_gather(hidden_out, mp_count)
    normed_next = layer_norm(whole_hidden, next_gain, next_bias).astype(jnp.bfloat16)
    next_raw = row_folder(
        normed_next, empty_sum, w_next_full
    )
    next_qkv = (
        (next_raw + next_qkv_bias.reshape(1, 3 * col_width))
        .astype(jnp.bfloat16)
        .reshape(tok_count, 3, col_width)
    )
    return (hidden_out, next_qkv)


def solution(mesh):
    in_specs = (
        P("pool", "mp"),
        P("pool", None),
        P(),
        P(),
        P("pool", None, "mp"),
        P(None, "mp"),
        P("pool", None, None, "mp"),
        P("mp", "pool"),
        P(),
        P(),
        P(),
        P("pool", None, "mp"),
        P(None, "mp"),
        P("pool"),
        P("pool"),
        P("pool", None),
    )
    out_specs = (P("pool", "mp"), P("pool", None, "mp"))
    return jax.shard_map(local, mesh=mesh, in_specs=in_specs, out_specs=out_specs, check_vma=False)
```

```python
import jax
import jax.numpy as jnp
from jax import lax
from jax.sharding import PartitionSpec as P
from jax.experimental import pallas as pl
from jax.experimental.pallas import tpu as pltpu

HEAD_DIM = 64
ROT = 32


epsilon = 1e-05


def layer_norm(row_data, gain_vec, bias_vec):
    values = row_data.astype(jnp.float32)
    row_mean = jnp.mean(values, axis=-1, keepdims=True)
    centered = values - row_mean
    spread = jnp.mean(centered * centered, axis=-1, keepdims=True)
    return centered * lax.rsqrt(spread + epsilon) * gain_vec + bias_vec


def rotate(head_rows, positions):
    half_rot = ROT // 2
    inverse = 10000.0 ** (-2.0 * jnp.arange(half_rot, dtype=jnp.float32) / ROT)
    angles = positions.astype(jnp.float32)[:, None] * inverse[None, :]
    cosine = jnp.cos(angles)[:, None, :]
    sine = jnp.sin(angles)[:, None, :]
    lower = head_rows[..., :half_rot]
    upper = head_rows[..., half_rot:ROT]
    return jnp.concatenate(
        [lower * cosine - upper * sine, upper * cosine + lower * sine, head_rows[..., ROT:]],
        axis=-1,
    )


def run_starts(token_request):
    tok_total = token_request.shape[0]
    token_index = jnp.arange(tok_total, dtype=jnp.int32)
    change = jnp.concatenate([jnp.ones((1,), dtype=bool), token_request[1:] != token_request[:-1]])
    return (token_index, lax.cummax(jnp.where(change, token_index, 0), axis=0))


def row_folder(left_rows, running, w_piece):
    columns_part = lax.slice_in_dim(left_rows, 0, w_piece.shape[0], axis=1)
    return running + jnp.dot(
        columns_part, w_piece.reshape(w_piece.shape[0], -1), preferred_element_type=jnp.float32
    )


def mp_gather(block, mp_count):
    spread = jnp.broadcast_to(block[None], (mp_count,) + block.shape)
    joined = lax.all_to_all(spread, "mp", split_axis=0, concat_axis=2, tiled=True)
    return joined.reshape(block.shape[0], mp_count * block.shape[1])


def mp_permute_gather(block, mp_count):
    mp_index = lax.axis_index("mp")
    moved = [block] + [
        lax.ppermute(block, "mp", [(src, (src + shift) % mp_count) for src in range(mp_count)])
        for shift in range(1, mp_count)
    ]
    stacked = jnp.stack(moved)
    by_source = stacked[(mp_index - jnp.arange(mp_count)) % mp_count]
    return by_source.transpose(1, 0, 2).reshape(block.shape[0], mp_count * block.shape[1])


Q_CHUNK = 256
PAIR = 128


def attention_body(q_ref, kc_ref, vc_ref, kn_ref, vn_ref, keyc_ref, keyn_ref, qreq_ref, out_ref):
    chunk = pl.program_id(1)
    n_slots = kc_ref.shape[0] * kc_ref.shape[1] * kc_ref.shape[2]
    n_new = kn_ref.shape[0]
    score_scale = HEAD_DIM ** (-0.5)
    q_req = qreq_ref[...]
    mask_c = q_req == keyc_ref[...]
    row_ids = chunk * Q_CHUNK + lax.broadcasted_iota(jnp.int32, (Q_CHUNK, n_new), 0)
    col_ids = lax.broadcasted_iota(jnp.int32, (Q_CHUNK, n_new), 1)
    mask_n = (q_req == keyn_ref[...]) & (col_ids <= row_ids)
    lane = lax.broadcasted_iota(jnp.int32, (1, PAIR), 1)
    nt = (((1,), (1,)), ((), ()))
    q_pair = q_ref[...]
    k_pair = kc_ref[...].reshape(n_slots, PAIR)
    v_pair = vc_ref[...].reshape(n_slots, PAIR)
    kn_pair = kn_ref[...]
    vn_pair = vn_ref[...]
    halves = []
    for half in range(PAIR // HEAD_DIM):
        in_head = (lane >= half * HEAD_DIM) & (lane < (half + 1) * HEAD_DIM)
        q_head = jnp.where(in_head, q_pair, jnp.zeros_like(q_pair))
        s_c = lax.dot_general(q_head, k_pair, nt, preferred_element_type=jnp.float32)
        s_n = lax.dot_general(q_head, kn_pair, nt, preferred_element_type=jnp.float32)
        s_c = jnp.where(mask_c, s_c * score_scale, -1e30)
        s_n = jnp.where(mask_n, s_n * score_scale, -1e30)
        row_max = jnp.maximum(
            jnp.max(s_c, axis=1, keepdims=True), jnp.max(s_n, axis=1, keepdims=True)
        )
        w_c = jnp.exp(s_c - row_max)
        w_n = jnp.exp(s_n - row_max)
        total = jnp.sum(w_c, axis=1, keepdims=True) + jnp.sum(w_n, axis=1, keepdims=True)
        p_c = (w_c / total).astype(jnp.bfloat16)
        p_n = (w_n / total).astype(jnp.bfloat16)
        o = jnp.dot(p_c, v_pair, preferred_element_type=jnp.float32) + jnp.dot(
            p_n, vn_pair, preferred_element_type=jnp.float32
        )
        halves.append((in_head, o))
    merged = jnp.where(halves[0][0], halves[0][1], halves[1][1])
    out_ref[...] = merged.astype(out_ref.dtype)


def attention_call(query, arrived, key_new, value_new, key_req_c, key_req_n, q_req):
    tok, width = query.shape
    holders, per, _, blk, _ = arrived.shape
    n_slots = holders * per * blk
    grid = (width // PAIR, tok // Q_CHUNK)
    full = lambda p, c: (0, 0)
    return pl.pallas_call(
        attention_body,
        grid=grid,
        in_specs=[
            pl.BlockSpec((Q_CHUNK, PAIR), lambda p, c: (c, p)),
            pl.BlockSpec((holders, per, None, blk, PAIR), lambda p, c: (0, 0, 0, 0, p)),
            pl.BlockSpec((holders, per, None, blk, PAIR), lambda p, c: (0, 0, 1, 0, p)),
            pl.BlockSpec((tok, PAIR), lambda p, c: (0, p)),
            pl.BlockSpec((tok, PAIR), lambda p, c: (0, p)),
            pl.BlockSpec((1, n_slots), full),
            pl.BlockSpec((1, tok), full),
            pl.BlockSpec((Q_CHUNK, 1), lambda p, c: (c, 0)),
        ],
        out_specs=pl.BlockSpec((Q_CHUNK, PAIR), lambda p, c: (c, p)),
        out_shape=jax.ShapeDtypeStruct((tok, width), jnp.bfloat16),
    )(query, arrived, arrived, key_new, value_new, key_req_c, key_req_n, q_req)


def local(
    residual_in,
    mlp_branch,
    norm_gain,
    norm_bias,
    w_qkv,
    qkv_bias,
    cache_pool,
    w_dense,
    dense_bias,
    next_gain,
    next_bias,
    w_next,
    next_qkv_bias,
    token_request,
    cache_len,
    block_table,
):
    mp_count = lax.axis_size("mp")
    full_rows = mp_permute_gather(residual_in, mp_count)
    tok_count = full_rows.shape[0]
    col_width = w_qkv.shape[2]
    head_count = col_width // HEAD_DIM
    normed = layer_norm(full_rows, norm_gain, norm_bias).astype(jnp.bfloat16)
    empty_sum = jnp.zeros((tok_count, 3 * col_width), jnp.float32)
    w_rows = w_qkv.shape[0]
    dense_shard = w_dense.T
    joined = jnp.concatenate(
        [w_qkv.reshape(w_rows, -1), w_next.reshape(w_rows, -1), dense_shard], axis=1
    )
    gathered = lax.all_gather(joined, "pool", axis=0, tiled=True)
    qkv_cols = 3 * col_width
    w_qkv_full = gathered[:, :qkv_cols]
    w_next_full = gathered[:, qkv_cols : 2 * qkv_cols]
    pool_total = lax.axis_size("pool")
    w_dense_t = gathered[:, 2 * qkv_cols :]
    projected = row_folder(normed, empty_sum, w_qkv_full)
    projected = (projected + qkv_bias.reshape(1, 3 * col_width)).reshape(tok_count, 3, col_width)
    token_index, starts = run_starts(token_request)
    request_count = cache_len.shape[0]
    local_req = token_request - request_count * lax.axis_index("pool")
    request_ids = jnp.arange(request_count, dtype=jnp.int32)
    request_match = local_req[:, None] == request_ids[None, :]
    cached_here = jnp.sum(jnp.where(request_match, cache_len[None, :], 0), axis=1)
    positions = cached_here + token_index - starts
    query = rotate(projected[:, 0].reshape(tok_count, head_count, HEAD_DIM), positions).astype(
        jnp.bfloat16
    )
    key_new = rotate(projected[:, 1].reshape(tok_count, head_count, HEAD_DIM), positions).astype(
        jnp.bfloat16
    )
    value_new = projected[:, 2].reshape(tok_count, head_count, HEAD_DIM).astype(jnp.bfloat16)
    pool_count = lax.axis_size("pool")
    blocks_here = cache_pool.shape[0]
    entries = block_table.reshape(-1)
    holder = entries // blocks_here
    entry_ids = jnp.arange(entries.shape[0], dtype=jnp.int32)
    earlier_same = (holder[:, None] == holder[None, :]) & (entry_ids[None, :] < entry_ids[:, None])
    per_holder = entries.shape[0] // pool_count
    slot_of = holder * per_holder + jnp.sum(earlier_same.astype(jnp.int32), axis=1)
    placed = slot_of[:, None] == entry_ids[None, :]
    holder_order = jnp.sum(jnp.where(placed, entry_ids[:, None], 0), axis=0)
    slot_ids = jnp.sum(jnp.where(placed, (entries % blocks_here)[:, None], 0), axis=0).reshape(
        pool_count, -1
    )
    wanted = lax.all_to_all(slot_ids, "pool", split_axis=0, concat_axis=0, tiled=True)
    packed = cache_pool[wanted.reshape(-1)].reshape((pool_count, -1) + cache_pool.shape[1:])
    arrived = lax.all_to_all(packed, "pool", split_axis=0, concat_axis=0, tiled=True)
    span = block_table.shape[1] * cache_pool.shape[2]
    blk_len = cache_pool.shape[2]
    entry_of = holder_order.astype(jnp.int32)
    entry_req = entry_of // block_table.shape[1]
    entry_lim = cache_len[entry_req] - (entry_of % block_table.shape[1]) * blk_len
    pos_in_blk = jnp.arange(blk_len, dtype=jnp.int32)
    key_req_c = jnp.where(
        pos_in_blk[None, :] < entry_lim[:, None], entry_req[:, None], -1
    ).reshape(1, -1)
    attended = attention_call(
        query.reshape(tok_count, col_width),
        arrived,
        key_new.reshape(tok_count, col_width),
        value_new.reshape(tok_count, col_width),
        key_req_c,
        local_req.reshape(1, tok_count),
        local_req.reshape(tok_count, 1),
    )
    partial_out = lax.dot_general(
        attended, w_dense_t, (((1,), (1,)), ((), ())), preferred_element_type=jnp.float32
    )
    mp_index = lax.axis_index("mp")
    pieces = partial_out.astype(jnp.bfloat16).reshape(tok_count, mp_count, col_width)
    arrived_sums = lax.all_to_all(pieces, "mp", split_axis=1, concat_axis=1, tiled=True)
    dense_total = jnp.sum(arrived_sums.astype(jnp.float32), axis=1)
    own_cols = lambda vec: lax.dynamic_slice_in_dim(vec, mp_index * col_width, col_width, 0)
    own_mlp = lax.dynamic_slice_in_dim(mlp_branch, mp_index * col_width, col_width, 1)
    hidden_out = (
        residual_in.astype(jnp.float32)
        + dense_total
        + own_cols(dense_bias)
        + own_mlp.astype(jnp.float32)
    ).astype(jnp.bfloat16)
    whole_hidden = mp_gather(hidden_out, mp_count)
    normed_next = layer_norm(whole_hidden, next_gain, next_bias).astype(jnp.bfloat16)
    next_raw = row_folder(
        normed_next, empty_sum, w_next_full
    )
    next_qkv = (
        (next_raw + next_qkv_bias.reshape(1, 3 * col_width))
        .astype(jnp.bfloat16)
        .reshape(tok_count, 3, col_width)
    )
    return (hidden_out, next_qkv)


def solution(mesh):
    in_specs = (
        P("pool", "mp"),
        P("pool", None),
        P(),
        P(),
        P("pool", None, "mp"),
        P(None, "mp"),
        P("pool", None, None, "mp"),
        P("mp", "pool"),
        P(),
        P(),
        P(),
        P("pool", None, "mp"),
        P(None, "mp"),
        P("pool"),
        P("pool"),
        P("pool", None),
    )
    out_specs = (P("pool", "mp"), P("pool", None, "mp"))
    return jax.shard_map(local, mesh=mesh, in_specs=in_specs, out_specs=out_specs, check_vma=False)
```

```python
import jax
import jax.numpy as jnp
from jax import lax
from jax.sharding import PartitionSpec as P
from jax.experimental import pallas as pl
from jax.experimental.pallas import tpu as pltpu

HEAD_DIM = 64
ROT = 32


epsilon = 1e-05


def layer_norm(row_data, gain_vec, bias_vec):
    values = row_data.astype(jnp.float32)
    row_mean = jnp.mean(values, axis=-1, keepdims=True)
    centered = values - row_mean
    spread = jnp.mean(centered * centered, axis=-1, keepdims=True)
    return centered * lax.rsqrt(spread + epsilon) * gain_vec + bias_vec


def rotate(head_rows, positions):
    half_rot = ROT // 2
    inverse = 10000.0 ** (-2.0 * jnp.arange(half_rot, dtype=jnp.float32) / ROT)
    angles = positions.astype(jnp.float32)[:, None] * inverse[None, :]
    cosine = jnp.cos(angles)[:, None, :]
    sine = jnp.sin(angles)[:, None, :]
    lower = head_rows[..., :half_rot]
    upper = head_rows[..., half_rot:ROT]
    return jnp.concatenate(
        [lower * cosine - upper * sine, upper * cosine + lower * sine, head_rows[..., ROT:]],
        axis=-1,
    )


def run_starts(token_request):
    tok_total = token_request.shape[0]
    token_index = jnp.arange(tok_total, dtype=jnp.int32)
    change = jnp.concatenate([jnp.ones((1,), dtype=bool), token_request[1:] != token_request[:-1]])
    return (token_index, lax.cummax(jnp.where(change, token_index, 0), axis=0))


def row_folder(left_rows, running, w_piece):
    columns_part = lax.slice_in_dim(left_rows, 0, w_piece.shape[0], axis=1)
    return running + jnp.dot(
        columns_part, w_piece.reshape(w_piece.shape[0], -1), preferred_element_type=jnp.float32
    )


def mp_gather(block, mp_count):
    spread = jnp.broadcast_to(block[None], (mp_count,) + block.shape)
    joined = lax.all_to_all(spread, "mp", split_axis=0, concat_axis=2, tiled=True)
    return joined.reshape(block.shape[0], mp_count * block.shape[1])


def mp_permute_gather(block, mp_count):
    mp_index = lax.axis_index("mp")
    moved = [block] + [
        lax.ppermute(block, "mp", [(src, (src + shift) % mp_count) for src in range(mp_count)])
        for shift in range(1, mp_count)
    ]
    stacked = jnp.stack(moved)
    by_source = stacked[(mp_index - jnp.arange(mp_count)) % mp_count]
    return by_source.transpose(1, 0, 2).reshape(block.shape[0], mp_count * block.shape[1])


Q_CHUNK = 256
PAIR = 128


def attention_body(q_ref, kc_ref, vc_ref, kn_ref, vn_ref, keyc_ref, keyn_ref, qreq_ref, wd_ref, out_ref, acc_ref):
    chunk = pl.program_id(1)
    n_slots = kc_ref.shape[0] * kc_ref.shape[1] * kc_ref.shape[2]
    n_new = kn_ref.shape[0]
    score_scale = HEAD_DIM ** (-0.5)
    q_req = qreq_ref[...]
    mask_c = q_req == keyc_ref[...]
    row_ids = chunk * Q_CHUNK + lax.broadcasted_iota(jnp.int32, (Q_CHUNK, n_new), 0)
    col_ids = lax.broadcasted_iota(jnp.int32, (Q_CHUNK, n_new), 1)
    mask_n = (q_req == keyn_ref[...]) & (col_ids <= row_ids)
    lane = lax.broadcasted_iota(jnp.int32, (1, PAIR), 1)
    nt = (((1,), (1,)), ((), ()))
    q_pair = q_ref[...]
    k_pair = kc_ref[...].reshape(n_slots, PAIR)
    v_pair = vc_ref[...].reshape(n_slots, PAIR)
    kn_pair = kn_ref[...]
    vn_pair = vn_ref[...]
    halves = []
    for half in range(PAIR // HEAD_DIM):
        in_head = (lane >= half * HEAD_DIM) & (lane < (half + 1) * HEAD_DIM)
        q_head = jnp.where(in_head, q_pair, jnp.zeros_like(q_pair))
        s_c = lax.dot_general(q_head, k_pair, nt, preferred_element_type=jnp.float32)
        s_n = lax.dot_general(q_head, kn_pair, nt, preferred_element_type=jnp.float32)
        s_c = jnp.where(mask_c, s_c * score_scale, -1e30)
        s_n = jnp.where(mask_n, s_n * score_scale, -1e30)
        row_max = jnp.maximum(
            jnp.max(s_c, axis=1, keepdims=True), jnp.max(s_n, axis=1, keepdims=True)
        )
        w_c = jnp.exp(s_c - row_max)
        w_n = jnp.exp(s_n - row_max)
        total = jnp.sum(w_c, axis=1, keepdims=True) + jnp.sum(w_n, axis=1, keepdims=True)
        p_c = (w_c / total).astype(jnp.bfloat16)
        p_n = (w_n / total).astype(jnp.bfloat16)
        o = jnp.dot(p_c, v_pair, preferred_element_type=jnp.float32) + jnp.dot(
            p_n, vn_pair, preferred_element_type=jnp.float32
        )
        halves.append((in_head, o))
    merged = jnp.where(halves[0][0], halves[0][1], halves[1][1]).astype(jnp.bfloat16)
    dense_part = lax.dot_general(merged, wd_ref[...], nt, preferred_element_type=jnp.float32)
    pair = pl.program_id(0)

    @pl.when(pair == 0)
    def _():
        acc_ref[...] = dense_part

    @pl.when(pair == pl.num_programs(0) - 1)
    def _():
        out_ref[...] = (acc_ref[...] + dense_part).astype(out_ref.dtype)


def attention_call(query, arrived, key_new, value_new, key_req_c, key_req_n, q_req, w_dense_t):
    tok, width = query.shape
    holders, per, _, blk, _ = arrived.shape
    n_slots = holders * per * blk
    grid = (width // PAIR, tok // Q_CHUNK)
    full = lambda p, c: (0, 0)
    return pl.pallas_call(
        attention_body,
        grid=grid,
        in_specs=[
            pl.BlockSpec((Q_CHUNK, PAIR), lambda p, c: (c, p)),
            pl.BlockSpec((holders, per, None, blk, PAIR), lambda p, c: (0, 0, 0, 0, p)),
            pl.BlockSpec((holders, per, None, blk, PAIR), lambda p, c: (0, 0, 1, 0, p)),
            pl.BlockSpec((tok, PAIR), lambda p, c: (0, p)),
            pl.BlockSpec((tok, PAIR), lambda p, c: (0, p)),
            pl.BlockSpec((1, n_slots), full),
            pl.BlockSpec((1, tok), full),
            pl.BlockSpec((Q_CHUNK, 1), lambda p, c: (c, 0)),
            pl.BlockSpec((w_dense_t.shape[0], PAIR), lambda p, c: (0, p)),
        ],
        out_specs=pl.BlockSpec((Q_CHUNK, w_dense_t.shape[0]), lambda p, c: (c, 0)),
        out_shape=jax.ShapeDtypeStruct((tok, w_dense_t.shape[0]), jnp.bfloat16),
        scratch_shapes=[pltpu.VMEM((Q_CHUNK, w_dense_t.shape[0]), jnp.float32)],
    )(query, arrived, arrived, key_new, value_new, key_req_c, key_req_n, q_req, w_dense_t)


def local(
    residual_in,
    mlp_branch,
    norm_gain,
    norm_bias,
    w_qkv,
    qkv_bias,
    cache_pool,
    w_dense,
    dense_bias,
    next_gain,
    next_bias,
    w_next,
    next_qkv_bias,
    token_request,
    cache_len,
    block_table,
):
    mp_count = lax.axis_size("mp")
    full_rows = mp_permute_gather(residual_in, mp_count)
    tok_count = full_rows.shape[0]
    col_width = w_qkv.shape[2]
    head_count = col_width // HEAD_DIM
    normed = layer_norm(full_rows, norm_gain, norm_bias).astype(jnp.bfloat16)
    empty_sum = jnp.zeros((tok_count, 3 * col_width), jnp.float32)
    w_rows = w_qkv.shape[0]
    dense_shard = w_dense.T
    joined = jnp.concatenate(
        [w_qkv.reshape(w_rows, -1), w_next.reshape(w_rows, -1), dense_shard], axis=1
    )
    gathered = lax.all_gather(joined, "pool", axis=0, tiled=True)
    qkv_cols = 3 * col_width
    w_qkv_full = gathered[:, :qkv_cols]
    w_next_full = gathered[:, qkv_cols : 2 * qkv_cols]
    pool_total = lax.axis_size("pool")
    w_dense_t = gathered[:, 2 * qkv_cols :]
    projected = row_folder(normed, empty_sum, w_qkv_full)
    projected = (projected + qkv_bias.reshape(1, 3 * col_width)).reshape(tok_count, 3, col_width)
    token_index, starts = run_starts(token_request)
    request_count = cache_len.shape[0]
    local_req = token_request - request_count * lax.axis_index("pool")
    request_ids = jnp.arange(request_count, dtype=jnp.int32)
    request_match = local_req[:, None] == request_ids[None, :]
    cached_here = jnp.sum(jnp.where(request_match, cache_len[None, :], 0), axis=1)
    positions = cached_here + token_index - starts
    query = rotate(projected[:, 0].reshape(tok_count, head_count, HEAD_DIM), positions).astype(
        jnp.bfloat16
    )
    key_new = rotate(projected[:, 1].reshape(tok_count, head_count, HEAD_DIM), positions).astype(
        jnp.bfloat16
    )
    value_new = projected[:, 2].reshape(tok_count, head_count, HEAD_DIM).astype(jnp.bfloat16)
    pool_count = lax.axis_size("pool")
    blocks_here = cache_pool.shape[0]
    entries = block_table.reshape(-1)
    holder = entries // blocks_here
    entry_ids = jnp.arange(entries.shape[0], dtype=jnp.int32)
    earlier_same = (holder[:, None] == holder[None, :]) & (entry_ids[None, :] < entry_ids[:, None])
    per_holder = entries.shape[0] // pool_count
    slot_of = holder * per_holder + jnp.sum(earlier_same.astype(jnp.int32), axis=1)
    placed = slot_of[:, None] == entry_ids[None, :]
    holder_order = jnp.sum(jnp.where(placed, entry_ids[:, None], 0), axis=0)
    slot_ids = jnp.sum(jnp.where(placed, (entries % blocks_here)[:, None], 0), axis=0).reshape(
        pool_count, -1
    )
    wanted = lax.all_to_all(slot_ids, "pool", split_axis=0, concat_axis=0, tiled=True)
    packed = cache_pool[wanted.reshape(-1)].reshape((pool_count, -1) + cache_pool.shape[1:])
    arrived = lax.all_to_all(packed, "pool", split_axis=0, concat_axis=0, tiled=True)
    span = block_table.shape[1] * cache_pool.shape[2]
    blk_len = cache_pool.shape[2]
    entry_of = holder_order.astype(jnp.int32)
    entry_req = entry_of // block_table.shape[1]
    entry_lim = cache_len[entry_req] - (entry_of % block_table.shape[1]) * blk_len
    pos_in_blk = jnp.arange(blk_len, dtype=jnp.int32)
    key_req_c = jnp.where(
        pos_in_blk[None, :] < entry_lim[:, None], entry_req[:, None], -1
    ).reshape(1, -1)
    attended = attention_call(
        query.reshape(tok_count, col_width),
        arrived,
        key_new.reshape(tok_count, col_width),
        value_new.reshape(tok_count, col_width),
        key_req_c,
        local_req.reshape(1, tok_count),
        local_req.reshape(tok_count, 1),
        w_dense_t,
    )
    mp_index = lax.axis_index("mp")
    pieces = attended.reshape(tok_count, mp_count, col_width)
    arrived_sums = lax.all_to_all(pieces, "mp", split_axis=1, concat_axis=1, tiled=True)
    dense_total = jnp.sum(arrived_sums.astype(jnp.float32), axis=1)
    own_cols = lambda vec: lax.dynamic_slice_in_dim(vec, mp_index * col_width, col_width, 0)
    own_mlp = lax.dynamic_slice_in_dim(mlp_branch, mp_index * col_width, col_width, 1)
    hidden_out = (
        residual_in.astype(jnp.float32)
        + dense_total
        + own_cols(dense_bias)
        + own_mlp.astype(jnp.float32)
    ).astype(jnp.bfloat16)
    whole_hidden = mp_gather(hidden_out, mp_count)
    normed_next = layer_norm(whole_hidden, next_gain, next_bias).astype(jnp.bfloat16)
    next_raw = row_folder(
        normed_next, empty_sum, w_next_full
    )
    next_qkv = (
        (next_raw + next_qkv_bias.reshape(1, 3 * col_width))
        .astype(jnp.bfloat16)
        .reshape(tok_count, 3, col_width)
    )
    return (hidden_out, next_qkv)


def solution(mesh):
    in_specs = (
        P("pool", "mp"),
        P("pool", None),
        P(),
        P(),
        P("pool", None, "mp"),
        P(None, "mp"),
        P("pool", None, None, "mp"),
        P("mp", "pool"),
        P(),
        P(),
        P(),
        P("pool", None, "mp"),
        P(None, "mp"),
        P("pool"),
        P("pool"),
        P("pool", None),
    )
    out_specs = (P("pool", "mp"), P("pool", None, "mp"))
    return jax.shard_map(local, mesh=mesh, in_specs=in_specs, out_specs=out_specs, check_vma=False)
```
